32 devices in a mesh: job: 2 (over x), space: 4 (over y, core), arc: 4 (over z).
Axes of the slice: x: 2, y: 2, z: 4, core: 2. Of those that a mesh axis runs over, the one named last changes fastest.
Arguments:
- saved_velocity_trajectory: bfloat16 [64, 3, 8, 128, 128], P(('job', 'arc'), None, 'space'), parts along dimension 0, may hold values from -4 to 4
- saved_warmth_trajectory: bfloat16 [64, 8, 128, 128], P(('job', 'arc'), 'space'), parts along dimension 0, may hold values from -5 to 5
- control_porosity: float32 [16, 128, 128], P(('job', 'space')), parts along dimension 0, may hold values from 0.05 to 1
- control_volume_flag: int32 [16, 128, 128], P(('job', 'space')), parts along dimension 0, may hold values 0 or 1
- entrance_face_flag: int32 [256, 128], P('job'), parts along dimension 0, may hold values 0 or 1
Outputs:
- gradient: float32 [16, 128, 128], P(('job', 'space'), 'arc'), parts along dimension 0
- entry_adjoint: float32 [8, 4, 8, 128, 128], P(('job', 'arc'), None, 'space'), parts along dimension 0
The draws below stay inside these ranges and needn't reach their ends.
There are 2 independent parts, one for each index of `job`. The reference program is written for one: setup_inputs(seed, part) draws one part's arguments, and reference() takes and returns one part's arrays. A program takes and returns all parts, laid end to end along the dimension named above; each array names one. Nothing has to cross between parts.
All inputs are finite; a program needn't handle non-finite values. No bound on the sum of `control_volume_flag` on one device may be relied on, other than what follows from the above.
Results may differ from the reference program's by a relative error of at most 0.0003.
Values may be sent and summed in bfloat16 or wider, within the bound.
No kernel may reach another device: no remote copies, remote signals or barrier semaphores. Data moves between devices by JAX's collectives and lax.ppermute only.
A program may use at most 64 MiB of HBM per device.

```python
import jax
import jax.numpy as jnp

MESH_SPAN_NORTH = 128
MESH_SPAN_UPWARD = 128
STEPS = 8
ARCS = 4
TIME_LEVELS = 32
MESH_SPAN_EAST = 8


def with_ends(array, key, least, top_value):
    shape = array.shape
    index_at = [jax.random.randint(jax.random.fold_in(key, axis), (), 0, shape[axis]) for axis in range(len(shape))]
    array = array.at[tuple(index_at)].set(least)
    longest = shape.index(max(shape))
    index_at[longest] = (index_at[longest] + 1) % shape[longest]
    return array.at[tuple(index_at)].set(top_value)


def level_of(own_key, dims, pieces, least, largest):
    def one(position, blocks):
        steps = jax.random.uniform(jax.random.fold_in(jax.random.fold_in(own_key, 6), position), (blocks,), jnp.float32, least / len(pieces), largest / len(pieces))
        return jnp.repeat(jnp.exp(steps), dims[position] // blocks).reshape((-1,) + (1,) * (len(dims) - position - 1))

    gain = one(*pieces[0])
    for cut in pieces[1:]:
        gain = gain * one(*cut)
    return gain


def normal_values(key, shape, deviation, most, shards=(), held_as=jnp.bfloat16):
    values = jax.random.normal(key, shape, jnp.float32) * deviation
    if len(shards) > 0:
        values = level_of(key, shape, shards, -0.22, 0.18) * values
    return jnp.clip(values, min=-most, max=most).astype(held_as)


def setup_inputs(seed: int = 0, part: int = 0) -> dict:
    splits = jax.random.split(jax.random.key(seed), 6)
    part_keys = jax.random.split(jax.random.fold_in(splits[5], part), 6)
    return {
        "saved_velocity_trajectory": normal_values(part_keys[0], (TIME_LEVELS, 3, MESH_SPAN_EAST, MESH_SPAN_NORTH, MESH_SPAN_UPWARD), 1.0, 4.0, ((0, 4), (2, 4))),
        "saved_warmth_trajectory": normal_values(part_keys[1], (TIME_LEVELS, MESH_SPAN_EAST, MESH_SPAN_NORTH, MESH_SPAN_UPWARD), 1.0, 5.0, ((0, 4), (1, 4))),
        "control_porosity": jnp.clip(0.05 + 0.95 * jax.random.uniform(part_keys[2], (MESH_SPAN_EAST, MESH_SPAN_NORTH, MESH_SPAN_UPWARD), jnp.float32) ** level_of(part_keys[2], (MESH_SPAN_EAST, MESH_SPAN_NORTH, MESH_SPAN_UPWARD), ((0, 4),), -0.2, 0.2), 0.05, 1.0),
        "control_volume_flag": with_ends((jax.random.randint(part_keys[3], (MESH_SPAN_EAST, MESH_SPAN_NORTH, MESH_SPAN_UPWARD), 0, 4) < 3).astype(jnp.int32), jax.random.fold_in(part_keys[3], 1), 0, 1),
        "entrance_face_flag": with_ends((jax.random.randint(part_keys[4], (MESH_SPAN_NORTH, MESH_SPAN_UPWARD), 0, 2) < 1).astype(jnp.int32), jax.random.fold_in(part_keys[4], 1), 0, 1),
    }


def laplace(ext):
    mid = ext[..., 1:-1, 1:-1, 1:-1]
    total = ext[..., 2:, 1:-1, 1:-1] + ext[..., :-2, 1:-1, 1:-1]
    total = total + ext[..., 1:-1, 2:, 1:-1] + ext[..., 1:-1, :-2, 1:-1]
    total = total + ext[..., 1:-1, 1:-1, 2:] + ext[..., 1:-1, 1:-1, :-2]
    return total - 6.0 * mid


def slopes(ext):
    return (0.5 * (ext[..., 2:, 1:-1, 1:-1] - ext[..., :-2, 1:-1, 1:-1]),
            0.5 * (ext[..., 1:-1, 2:, 1:-1] - ext[..., 1:-1, :-2, 1:-1]),
            0.5 * (ext[..., 1:-1, 1:-1, 2:] - ext[..., 1:-1, 1:-1, :-2]))


def pad_sides(field, operating_variant):
    widths = [(0, 0)] * (field.ndim - 2) + [(1, 1), (1, 1)]
    return jnp.pad(field, widths, mode=operating_variant)


def adjoint_update(adj, ext_a, ext_b, padded_thermal_field, speed, alpha, porosity_sensitivity, solid, quadrature_factor):
    a_now = adj[:3]
    current_adjoint_vector = adj[3]
    grad_b = slopes(ext_b)
    grad_a = slopes(ext_a)
    grad_t = slopes(padded_thermal_field)
    carry_b = speed[0] * grad_b[0] + speed[1] * grad_b[1] + speed[2] * grad_b[2]
    carry_a = speed[0:1] * grad_a[0] + speed[1:2] * grad_a[1] + speed[2:3] * grad_a[2]
    thermal_current_field = padded_thermal_field[1:-1, 1:-1, 1:-1]
    grad_stack = jnp.stack(grad_t)
    new_a = a_now + 0.1 * (1.2 * laplace(ext_a) + carry_a - alpha * a_now - current_adjoint_vector * grad_stack)
    new_b = current_adjoint_vector + 0.1 * (1.2 * laplace(ext_b) + carry_b - 2.0 * solid * current_adjoint_vector + 2.0 * solid)
    common_divisor_lcm_like = jnp.sum(a_now * speed, axis=0)
    summand_contribution = 0.1 * quadrature_factor * (porosity_sensitivity * common_divisor_lcm_like + 2.0 * (current_adjoint_vector - 1.0) * thermal_current_field)
    return jnp.concatenate([new_a, new_b[None]], axis=0), summand_contribution


def reference(saved_velocity_trajectory, saved_warmth_trajectory, control_porosity, control_volume_flag, entrance_face_flag):
    quadrature_factor = control_volume_flag.astype(jnp.float32)
    gamma = jnp.where(control_volume_flag == 1, control_porosity, jnp.float32(0.0))
    solid = 1.0 - gamma
    alpha = 3.0 * 0.1 * solid / (0.1 + gamma)
    porosity_sensitivity = -3.0 * 0.1 * 1.1 / ((0.1 + gamma) * (0.1 + gamma))

    def one_step(adj, instant_number):
        speed = saved_velocity_trajectory[instant_number].astype(jnp.float32)
        thermal_current_field = saved_warmth_trajectory[instant_number].astype(jnp.float32)
        padded_thermal_field = jnp.pad(thermal_current_field, 1, mode="edge")
        ext_a = jnp.pad(adj[:3], ((0, 0), (1, 1), (1, 1), (1, 1)))
        current_adjoint_vector = adj[3]
        floor_limit = jnp.where(entrance_face_flag == 1, jnp.float32(0.0), current_adjoint_vector[0])
        ceiling_bound = current_adjoint_vector[-1]
        ext_b = pad_sides(jnp.concatenate([floor_limit[None], current_adjoint_vector, ceiling_bound[None]], axis=0), "edge")
        return adjoint_update(adj, ext_a, ext_b, padded_thermal_field, speed, alpha, porosity_sensitivity, solid, quadrature_factor)

    grid_shape = (4,) + control_porosity.shape
    firsts = []
    for arc in range(ARCS):
        adj = jnp.zeros(grid_shape, jnp.float32)
        for interior_block in range(STEPS - 1, -1, -1):
            adj, unused = one_step(adj, arc * STEPS + interior_block)
        firsts.append(adj)
    gradient = jnp.zeros(control_porosity.shape, jnp.float32)
    entries = []
    for arc in range(ARCS):
        adj = firsts[(arc + 1) % ARCS]
        for interior_block in range(STEPS - 1, -1, -1):
            adj, summand_contribution = one_step(adj, arc * STEPS + interior_block)
            gradient = gradient + summand_contribution
        entries.append(adj)
    return gradient, jnp.stack(entries)
```

```python
import jax
import jax.numpy as jnp
from jax import lax
from jax.sharding import PartitionSpec as P


def padded(cells, sides, width):
    for axis, dim in sides:
        count = lax.axis_size(axis)
        ends = count - 1
        head = lax.slice_in_dim(cells, 0, width, axis=dim)
        tail = lax.slice_in_dim(cells, cells.shape[dim] - width, cells.shape[dim], axis=dim)
        cells = jnp.concatenate(
            [
                lax.ppermute(tail, axis, [(i, (i + 1) % count) for i in range(ends)]),
                cells,
                lax.ppermute(head, axis, [((i + 1) % count, i) for i in range(ends)]),
            ],
            axis=dim,
        )
    return cells


def passed_along(value, axis, steps):
    count = lax.axis_size(axis)
    pairs = [(source, (source + steps) % count) for source in range(count)]
    return lax.ppermute(value, axis, pairs)


def laplace(ext):
    mid = ext[..., 1:-1, 1:-1, 1:-1]
    total = ext[..., 2:, 1:-1, 1:-1] + ext[..., :-2, 1:-1, 1:-1]
    total = total + ext[..., 1:-1, 2:, 1:-1] + ext[..., 1:-1, :-2, 1:-1]
    total = total + ext[..., 1:-1, 1:-1, 2:] + ext[..., 1:-1, 1:-1, :-2]
    return total - 6.0 * mid


def slopes(ext):
    return (
        0.5 * (ext[..., 2:, 1:-1, 1:-1] - ext[..., :-2, 1:-1, 1:-1]),
        0.5 * (ext[..., 1:-1, 2:, 1:-1] - ext[..., 1:-1, :-2, 1:-1]),
        0.5 * (ext[..., 1:-1, 1:-1, 2:] - ext[..., 1:-1, 1:-1, :-2]),
    )


def pad_sides(field, operating_variant):
    widths = [(0, 0)] * (field.ndim - 2) + [(1, 1), (1, 1)]
    return jnp.pad(field, widths, mode=operating_variant)


def adjoint_update(
    adj,
    ext_a,
    ext_b,
    padded_thermal_field,
    speed,
    alpha,
    porosity_sensitivity,
    solid,
    quadrature_factor,
):
    a_now = adj[:3]
    current_adjoint_vector = adj[3]
    grad_b = slopes(ext_b)
    grad_a = slopes(ext_a)
    grad_t = slopes(padded_thermal_field)
    carry_b = speed[0] * grad_b[0] + speed[1] * grad_b[1] + speed[2] * grad_b[2]
    carry_a = speed[0:1] * grad_a[0] + speed[1:2] * grad_a[1] + speed[2:3] * grad_a[2]
    thermal_current_field = padded_thermal_field[1:-1, 1:-1, 1:-1]
    grad_stack = jnp.stack(grad_t)
    new_a = a_now + 0.1 * (
        1.2 * laplace(ext_a) + carry_a - alpha * a_now - current_adjoint_vector * grad_stack
    )
    new_b = current_adjoint_vector + 0.1 * (
        1.2 * laplace(ext_b) + carry_b - 2.0 * solid * current_adjoint_vector + 2.0 * solid
    )
    common_divisor_lcm_like = jnp.sum(a_now * speed, axis=0)
    summand_contribution = (
        0.1
        * quadrature_factor
        * (
            porosity_sensitivity * common_divisor_lcm_like
            + 2.0 * (current_adjoint_vector - 1.0) * thermal_current_field
        )
    )
    return (jnp.concatenate([new_a, new_b[None]], axis=0), summand_contribution)


def halo_body(
    saved_velocity_trajectory,
    saved_warmth_trajectory,
    control_porosity,
    control_volume_flag,
    entrance_face_flag,
):
    quadrature_factor = control_volume_flag.astype(jnp.float32)
    gamma = jnp.where(control_volume_flag == 1, control_porosity, jnp.float32(0.0))
    solid = 1.0 - gamma
    alpha = 3.0 * 0.1 * solid / (0.1 + gamma)
    porosity_sensitivity = -3.0 * 0.1 * 1.1 / ((0.1 + gamma) * (0.1 + gamma))
    leading_plane = lax.axis_index("space") == 0
    trailing_plane = lax.axis_index("space") == lax.axis_size("space") - 1
    device_instant_total = saved_warmth_trajectory.shape[0]
    cycle_ext = padded(saved_warmth_trajectory, (("space", 1),), 1)

    def closing_thermal_value(thermal_current_field, with_halo_padding):
        floor_limit = jnp.where(leading_plane, thermal_current_field[0], with_halo_padding[0])
        ceiling_bound = jnp.where(trailing_plane, thermal_current_field[-1], with_halo_padding[-1])
        return pad_sides(
            jnp.concatenate(
                [floor_limit[None], thermal_current_field, ceiling_bound[None]], axis=0
            ),
            "edge",
        )

    def one_step(adj, interior_block):
        speed = saved_velocity_trajectory[interior_block].astype(jnp.float32)
        thermal_current_field = saved_warmth_trajectory[interior_block].astype(jnp.float32)
        with_halo_padding = padded(adj, (("space", 1),), 1)
        thermal_halo_values = cycle_ext[interior_block].astype(jnp.float32)
        complete_thermal_field = jnp.concatenate(
            [thermal_halo_values[:1], thermal_current_field, thermal_halo_values[-1:]], axis=0
        )
        padded_thermal_field = closing_thermal_value(thermal_current_field, complete_thermal_field)
        ext_a = pad_sides(with_halo_padding[:3], "constant")
        current_adjoint_vector = adj[3]
        floor_limit = jnp.where(
            leading_plane,
            jnp.where(entrance_face_flag == 1, jnp.float32(0.0), current_adjoint_vector[0]),
            with_halo_padding[3, 0],
        )
        ceiling_bound = jnp.where(
            trailing_plane, current_adjoint_vector[-1], with_halo_padding[3, -1]
        )
        ext_b = pad_sides(
            jnp.concatenate(
                [floor_limit[None], current_adjoint_vector, ceiling_bound[None]], axis=0
            ),
            "edge",
        )
        return adjoint_update(
            adj,
            ext_a,
            ext_b,
            padded_thermal_field,
            speed,
            alpha,
            porosity_sensitivity,
            solid,
            quadrature_factor,
        )

    grid_shape = (4,) + control_porosity.shape
    adj = jnp.zeros(grid_shape, jnp.float32)
    for interior_block in range(device_instant_total - 1, -1, -1):
        adj, unused = one_step(adj, interior_block)
    adj = passed_along(adj, "arc", -1)
    partial_sum = jnp.zeros(control_porosity.shape, jnp.float32)
    for interior_block in range(device_instant_total - 1, -1, -1):
        adj, summand_contribution = one_step(adj, interior_block)
        partial_sum = partial_sum + summand_contribution
    summed = lax.psum(partial_sum, "arc")
    share = summed.shape[1] // lax.axis_size("arc")
    gradient = lax.dynamic_slice_in_dim(summed, lax.axis_index("arc") * share, share, 1)
    return (gradient, adj[None])


def whole_grid_body(
    saved_velocity_trajectory,
    saved_warmth_trajectory,
    control_porosity,
    control_volume_flag,
    entrance_face_flag,
):
    lanes = saved_warmth_trajectory.shape[1]
    steps = saved_warmth_trajectory.shape[0]
    me = lax.axis_index("space")

    stacked = jnp.concatenate(
        [saved_velocity_trajectory, saved_warmth_trajectory[:, None]], axis=1
    )
    inputs_all = [None] * steps
    for s in range(steps - 1, -1, -1):
        inputs_all[s] = lax.all_gather(stacked[s], "space", axis=1, tiled=True)

    own_gamma = jnp.where(control_volume_flag == 1, control_porosity, jnp.float32(0.0))
    gamma = lax.all_gather(own_gamma, "space", axis=0, tiled=True)
    solid = 1.0 - gamma
    alpha = 3.0 * 0.1 * solid / (0.1 + gamma)
    own_flag = control_volume_flag.astype(jnp.float32)
    own_sensitivity = -3.0 * 0.1 * 1.1 / ((0.1 + own_gamma) * (0.1 + own_gamma))

    def one_step(adj, s):
        speed = inputs_all[s][:3].astype(jnp.float32)
        thermal = inputs_all[s][3].astype(jnp.float32)
        padded_thermal = jnp.pad(thermal, 1, mode="edge")
        ext_a = jnp.pad(adj[:3], ((0, 0), (1, 1), (1, 1), (1, 1)))
        b = adj[3]
        floor_limit = jnp.where(entrance_face_flag == 1, jnp.float32(0.0), b[0])
        ext_b = pad_sides(jnp.concatenate([floor_limit[None], b, b[-1][None]], axis=0), "edge")
        a_now = adj[:3]
        grad_b = slopes(ext_b)
        grad_a = slopes(ext_a)
        grad_t = slopes(padded_thermal)
        carry_b = speed[0] * grad_b[0] + speed[1] * grad_b[1] + speed[2] * grad_b[2]
        carry_a = speed[0:1] * grad_a[0] + speed[1:2] * grad_a[1] + speed[2:3] * grad_a[2]
        new_a = a_now + 0.1 * (
            1.2 * laplace(ext_a) + carry_a - alpha * a_now - b * jnp.stack(grad_t)
        )
        new_b = b + 0.1 * (1.2 * laplace(ext_b) + carry_b - 2.0 * solid * b + 2.0 * solid)
        return jnp.concatenate([new_a, new_b[None]], axis=0)

    def own_cells(x, axis):
        return lax.dynamic_slice_in_dim(x, me * lanes, lanes, axis)

    def sensitivity(adj, s):
        a_loc = own_cells(adj[:3], 1)
        b_loc = own_cells(adj[3], 0)
        speed = saved_velocity_trajectory[s].astype(jnp.float32)
        thermal = saved_warmth_trajectory[s].astype(jnp.float32)
        dot = jnp.sum(a_loc * speed, axis=0)
        return 0.1 * own_flag * (own_sensitivity * dot + 2.0 * (b_loc - 1.0) * thermal)

    grid_shape = (4,) + gamma.shape
    adj = jnp.zeros(grid_shape, jnp.float32)
    for s in range(steps - 1, -1, -1):
        adj = one_step(adj, s)

    core = me % 2
    half = adj.shape[0] // 2
    mine = lax.dynamic_slice_in_dim(adj, core * half, half, 0)
    arrived = passed_along(mine, "arc", -1)
    space_count = lax.axis_size("space")
    swap = [(i, i ^ 1) for i in range(space_count)]
    other = lax.ppermute(arrived, "space", swap)
    adj = jnp.where(
        core == 0,
        jnp.concatenate([arrived, other], axis=0),
        jnp.concatenate([other, arrived], axis=0),
    )

    partial_sum = jnp.zeros(control_porosity.shape, jnp.float32)
    for s in range(steps - 1, -1, -1):
        partial_sum = partial_sum + sensitivity(adj, s)
        adj = one_step(adj, s)

    arcs = lax.axis_size("arc")
    k = lax.axis_index("arc")
    share = partial_sum.shape[1] // arcs
    pieces = partial_sum.reshape(partial_sum.shape[0], arcs, share, partial_sum.shape[2])
    total = lax.dynamic_index_in_dim(pieces, k, 1, keepdims=False)
    for shift in range(1, arcs):
        piece = lax.dynamic_index_in_dim(pieces, (k + shift) % arcs, 1, keepdims=False)
        total = total + passed_along(piece, "arc", shift)
    entry = own_cells(adj, 1)
    return (total, entry[None])


def solution(mesh):
    chosen = whole_grid_body if mesh.shape["space"] <= 4 else halo_body
    return jax.shard_map(
        chosen,
        mesh=mesh,
        in_specs=(
            P(("job", "arc"), None, "space", None, None),
            P(("job", "arc"), "space", None, None),
            P(("job", "space"), None, None),
            P(("job", "space"), None, None),
            P("job", None),
        ),
        out_specs=(P(("job", "space"), "arc", None), P(("job", "arc"), None, "space", None, None)),
        check_vma=False,
    )
```

```python
import jax
import jax.numpy as jnp
from jax import lax
from jax.sharding import PartitionSpec as P


def padded(cells, sides, width):
    for axis, dim in sides:
        count = lax.axis_size(axis)
        ends = count - 1
        head = lax.slice_in_dim(cells, 0, width, axis=dim)
        tail = lax.slice_in_dim(cells, cells.shape[dim] - width, cells.shape[dim], axis=dim)
        cells = jnp.concatenate(
            [
                lax.ppermute(tail, axis, [(i, (i + 1) % count) for i in range(ends)]),
                cells,
                lax.ppermute(head, axis, [((i + 1) % count, i) for i in range(ends)]),
            ],
            axis=dim,
        )
    return cells


def passed_along(value, axis, steps):
    count = lax.axis_size(axis)
    pairs = [(source, (source + steps) % count) for source in range(count)]
    return lax.ppermute(value, axis, pairs)


def laplace(ext):
    mid = ext[..., 1:-1, 1:-1, 1:-1]
    total = ext[..., 2:, 1:-1, 1:-1] + ext[..., :-2, 1:-1, 1:-1]
    total = total + ext[..., 1:-1, 2:, 1:-1] + ext[..., 1:-1, :-2, 1:-1]
    total = total + ext[..., 1:-1, 1:-1, 2:] + ext[..., 1:-1, 1:-1, :-2]
    return total - 6.0 * mid


def slopes(ext):
    return (
        0.5 * (ext[..., 2:, 1:-1, 1:-1] - ext[..., :-2, 1:-1, 1:-1]),
        0.5 * (ext[..., 1:-1, 2:, 1:-1] - ext[..., 1:-1, :-2, 1:-1]),
        0.5 * (ext[..., 1:-1, 1:-1, 2:] - ext[..., 1:-1, 1:-1, :-2]),
    )


def pad_sides(field, operating_variant):
    widths = [(0, 0)] * (field.ndim - 2) + [(1, 1), (1, 1)]
    return jnp.pad(field, widths, mode=operating_variant)


def adjoint_update(
    adj,
    ext_a,
    ext_b,
    padded_thermal_field,
    speed,
    alpha,
    porosity_sensitivity,
    solid,
    quadrature_factor,
):
    a_now = adj[:3]
    current_adjoint_vector = adj[3]
    grad_b = slopes(ext_b)
    grad_a = slopes(ext_a)
    grad_t = slopes(padded_thermal_field)
    carry_b = speed[0] * grad_b[0] + speed[1] * grad_b[1] + speed[2] * grad_b[2]
    carry_a = speed[0:1] * grad_a[0] + speed[1:2] * grad_a[1] + speed[2:3] * grad_a[2]
    thermal_current_field = padded_thermal_field[1:-1, 1:-1, 1:-1]
    grad_stack = jnp.stack(grad_t)
    new_a = a_now + 0.1 * (
        1.2 * laplace(ext_a) + carry_a - alpha * a_now - current_adjoint_vector * grad_stack
    )
    new_b = current_adjoint_vector + 0.1 * (
        1.2 * laplace(ext_b) + carry_b - 2.0 * solid * current_adjoint_vector + 2.0 * solid
    )
    common_divisor_lcm_like = jnp.sum(a_now * speed, axis=0)
    summand_contribution = (
        0.1
        * quadrature_factor
        * (
            porosity_sensitivity * common_divisor_lcm_like
            + 2.0 * (current_adjoint_vector - 1.0) * thermal_current_field
        )
    )
    return (jnp.concatenate([new_a, new_b[None]], axis=0), summand_contribution)


def halo_body(
    saved_velocity_trajectory,
    saved_warmth_trajectory,
    control_porosity,
    control_volume_flag,
    entrance_face_flag,
):
    quadrature_factor = control_volume_flag.astype(jnp.float32)
    gamma = jnp.where(control_volume_flag == 1, control_porosity, jnp.float32(0.0))
    solid = 1.0 - gamma
    alpha = 3.0 * 0.1 * solid / (0.1 + gamma)
    porosity_sensitivity = -3.0 * 0.1 * 1.1 / ((0.1 + gamma) * (0.1 + gamma))
    leading_plane = lax.axis_index("space") == 0
    trailing_plane = lax.axis_index("space") == lax.axis_size("space") - 1
    device_instant_total = saved_warmth_trajectory.shape[0]
    cycle_ext = padded(saved_warmth_trajectory, (("space", 1),), 1)

    def closing_thermal_value(thermal_current_field, with_halo_padding):
        floor_limit = jnp.where(leading_plane, thermal_current_field[0], with_halo_padding[0])
        ceiling_bound = jnp.where(trailing_plane, thermal_current_field[-1], with_halo_padding[-1])
        return pad_sides(
            jnp.concatenate(
                [floor_limit[None], thermal_current_field, ceiling_bound[None]], axis=0
            ),
            "edge",
        )

    def one_step(adj, interior_block):
        speed = saved_velocity_trajectory[interior_block].astype(jnp.float32)
        thermal_current_field = saved_warmth_trajectory[interior_block].astype(jnp.float32)
        with_halo_padding = padded(adj, (("space", 1),), 1)
        thermal_halo_values = cycle_ext[interior_block].astype(jnp.float32)
        complete_thermal_field = jnp.concatenate(
            [thermal_halo_values[:1], thermal_current_field, thermal_halo_values[-1:]], axis=0
        )
        padded_thermal_field = closing_thermal_value(thermal_current_field, complete_thermal_field)
        ext_a = pad_sides(with_halo_padding[:3], "constant")
        current_adjoint_vector = adj[3]
        floor_limit = jnp.where(
            leading_plane,
            jnp.where(entrance_face_flag == 1, jnp.float32(0.0), current_adjoint_vector[0]),
            with_halo_padding[3, 0],
        )
        ceiling_bound = jnp.where(
            trailing_plane, current_adjoint_vector[-1], with_halo_padding[3, -1]
        )
        ext_b = pad_sides(
            jnp.concatenate(
                [floor_limit[None], current_adjoint_vector, ceiling_bound[None]], axis=0
            ),
            "edge",
        )
        return adjoint_update(
            adj,
            ext_a,
            ext_b,
            padded_thermal_field,
            speed,
            alpha,
            porosity_sensitivity,
            solid,
            quadrature_factor,
        )

    grid_shape = (4,) + control_porosity.shape
    adj = jnp.zeros(grid_shape, jnp.float32)
    for interior_block in range(device_instant_total - 1, -1, -1):
        adj, unused = one_step(adj, interior_block)
    adj = passed_along(adj, "arc", -1)
    partial_sum = jnp.zeros(control_porosity.shape, jnp.float32)
    for interior_block in range(device_instant_total - 1, -1, -1):
        adj, summand_contribution = one_step(adj, interior_block)
        partial_sum = partial_sum + summand_contribution
    summed = lax.psum(partial_sum, "arc")
    share = summed.shape[1] // lax.axis_size("arc")
    gradient = lax.dynamic_slice_in_dim(summed, lax.axis_index("arc") * share, share, 1)
    return (gradient, adj[None])


def swap_over(value, partner_bit):
    count = lax.axis_size("space")
    return lax.ppermute(value, "space", [(i, i ^ partner_bit) for i in range(count)])


def gathered_cells(local, me, axis):
    far = swap_over(local, 2)
    both = jnp.stack([local, far])
    near = swap_over(both, 1)
    pieces = [both[0], near[0], both[1], near[1]]
    odd = (me & 1) == 1
    pieces = [
        jnp.where(odd, pieces[1], pieces[0]),
        jnp.where(odd, pieces[0], pieces[1]),
        jnp.where(odd, pieces[3], pieces[2]),
        jnp.where(odd, pieces[2], pieces[3]),
    ]
    high = (me & 2) == 2
    pieces = [
        jnp.where(high, pieces[2], pieces[0]),
        jnp.where(high, pieces[3], pieces[1]),
        jnp.where(high, pieces[0], pieces[2]),
        jnp.where(high, pieces[1], pieces[3]),
    ]
    return jnp.concatenate(pieces, axis=axis)


def whole_grid_body(
    saved_velocity_trajectory,
    saved_warmth_trajectory,
    control_porosity,
    control_volume_flag,
    entrance_face_flag,
):
    lanes = saved_warmth_trajectory.shape[1]
    steps = saved_warmth_trajectory.shape[0]
    me = lax.axis_index("space")

    stacked = jnp.concatenate(
        [saved_velocity_trajectory, saved_warmth_trajectory[:, None]], axis=1
    )
    inputs_all = [None] * steps
    chunk = 2 if steps % 2 == 0 else 1
    for top in range(steps, 0, -chunk):
        piece = gathered_cells(stacked[top - chunk:top], me, 2)
        for j in range(chunk):
            inputs_all[top - chunk + j] = piece[j]

    own_gamma = jnp.where(control_volume_flag == 1, control_porosity, jnp.float32(0.0))
    gamma = gathered_cells(own_gamma, me, 0)
    solid = 1.0 - gamma
    alpha = 3.0 * 0.1 * solid / (0.1 + gamma)
    own_flag = control_volume_flag.astype(jnp.float32)
    own_sensitivity = -3.0 * 0.1 * 1.1 / ((0.1 + own_gamma) * (0.1 + own_gamma))

    def one_step(adj, s):
        speed = inputs_all[s][:3].astype(jnp.float32)
        thermal = inputs_all[s][3].astype(jnp.float32)
        padded_thermal = jnp.pad(thermal, 1, mode="edge")
        ext_a = jnp.pad(adj[:3], ((0, 0), (1, 1), (1, 1), (1, 1)))
        b = adj[3]
        floor_limit = jnp.where(entrance_face_flag == 1, jnp.float32(0.0), b[0])
        ext_b = pad_sides(jnp.concatenate([floor_limit[None], b, b[-1][None]], axis=0), "edge")
        a_now = adj[:3]
        grad_b = slopes(ext_b)
        grad_a = slopes(ext_a)
        grad_t = slopes(padded_thermal)
        carry_b = speed[0] * grad_b[0] + speed[1] * grad_b[1] + speed[2] * grad_b[2]
        carry_a = speed[0:1] * grad_a[0] + speed[1:2] * grad_a[1] + speed[2:3] * grad_a[2]
        new_a = a_now + 0.1 * (
            1.2 * laplace(ext_a) + carry_a - alpha * a_now - b * jnp.stack(grad_t)
        )
        new_b = b + 0.1 * (1.2 * laplace(ext_b) + carry_b - 2.0 * solid * b + 2.0 * solid)
        return jnp.concatenate([new_a, new_b[None]], axis=0)

    def own_cells(x, axis):
        return lax.dynamic_slice_in_dim(x, me * lanes, lanes, axis)

    def sensitivity(adj, s):
        a_loc = own_cells(adj[:3], 1)
        b_loc = own_cells(adj[3], 0)
        speed = saved_velocity_trajectory[s].astype(jnp.float32)
        thermal = saved_warmth_trajectory[s].astype(jnp.float32)
        dot = jnp.sum(a_loc * speed, axis=0)
        return 0.1 * own_flag * (own_sensitivity * dot + 2.0 * (b_loc - 1.0) * thermal)

    grid_shape = (4,) + gamma.shape
    adj = jnp.zeros(grid_shape, jnp.float32)
    for s in range(steps - 1, -1, -1):
        adj = one_step(adj, s)

    core = me % 2
    half = adj.shape[0] // 2
    mine = lax.dynamic_slice_in_dim(adj, core * half, half, 0)
    arrived = passed_along(mine, "arc", -1)
    space_count = lax.axis_size("space")
    swap = [(i, i ^ 1) for i in range(space_count)]
    other = lax.ppermute(arrived, "space", swap)
    adj = jnp.where(
        core == 0,
        jnp.concatenate([arrived, other], axis=0),
        jnp.concatenate([other, arrived], axis=0),
    )

    partial_sum = jnp.zeros(control_porosity.shape, jnp.float32)
    for s in range(steps - 1, -1, -1):
        partial_sum = partial_sum + sensitivity(adj, s)
        adj = one_step(adj, s)

    arcs = lax.axis_size("arc")
    k = lax.axis_index("arc")
    share = partial_sum.shape[1] // arcs
    pieces = partial_sum.reshape(partial_sum.shape[0], arcs, share, partial_sum.shape[2])
    total = lax.dynamic_index_in_dim(pieces, k, 1, keepdims=False)
    for shift in range(1, arcs):
        piece = lax.dynamic_index_in_dim(pieces, (k + shift) % arcs, 1, keepdims=False)
        total = total + passed_along(piece, "arc", shift)
    entry = own_cells(adj, 1)
    return (total, entry[None])


def solution(mesh):
    chosen = whole_grid_body if mesh.shape["space"] == 4 else halo_body
    return jax.shard_map(
        chosen,
        mesh=mesh,
        in_specs=(
            P(("job", "arc"), None, "space", None, None),
            P(("job", "arc"), "space", None, None),
            P(("job", "space"), None, None),
            P(("job", "space"), None, None),
            P("job", None),
        ),
        out_specs=(P(("job", "space"), "arc", None), P(("job", "arc"), None, "space", None, None)),
        check_vma=False,
    )
```

```python
import jax
import jax.numpy as jnp
from jax import lax
from jax.sharding import PartitionSpec as P


def padded(cells, sides, width):
    for axis, dim in sides:
        count = lax.axis_size(axis)
        ends = count - 1
        head = lax.slice_in_dim(cells, 0, width, axis=dim)
        tail = lax.slice_in_dim(cells, cells.shape[dim] - width, cells.shape[dim], axis=dim)
        cells = jnp.concatenate(
            [
                lax.ppermute(tail, axis, [(i, (i + 1) % count) for i in range(ends)]),
                cells,
                lax.ppermute(head, axis, [((i + 1) % count, i) for i in range(ends)]),
            ],
            axis=dim,
        )
    return cells


def passed_along(value, axis, steps):
    count = lax.axis_size(axis)
    pairs = [(source, (source + steps) % count) for source in range(count)]
    return lax.ppermute(value, axis, pairs)


def laplace(ext):
    mid = ext[..., 1:-1, 1:-1, 1:-1]
    total = ext[..., 2:, 1:-1, 1:-1] + ext[..., :-2, 1:-1, 1:-1]
    total = total + ext[..., 1:-1, 2:, 1:-1] + ext[..., 1:-1, :-2, 1:-1]
    total = total + ext[..., 1:-1, 1:-1, 2:] + ext[..., 1:-1, 1:-1, :-2]
    return total - 6.0 * mid


def slopes(ext):
    return (
        0.5 * (ext[..., 2:, 1:-1, 1:-1] - ext[..., :-2, 1:-1, 1:-1]),
        0.5 * (ext[..., 1:-1, 2:, 1:-1] - ext[..., 1:-1, :-2, 1:-1]),
        0.5 * (ext[..., 1:-1, 1:-1, 2:] - ext[..., 1:-1, 1:-1, :-2]),
    )


def pad_sides(field, operating_variant):
    widths = [(0, 0)] * (field.ndim - 2) + [(1, 1), (1, 1)]
    return jnp.pad(field, widths, mode=operating_variant)


def adjoint_update(
    adj,
    ext_a,
    ext_b,
    padded_thermal_field,
    speed,
    alpha,
    porosity_sensitivity,
    solid,
    quadrature_factor,
):
    a_now = adj[:3]
    current_adjoint_vector = adj[3]
    grad_b = slopes(ext_b)
    grad_a = slopes(ext_a)
    grad_t = slopes(padded_thermal_field)
    carry_b = speed[0] * grad_b[0] + speed[1] * grad_b[1] + speed[2] * grad_b[2]
    carry_a = speed[0:1] * grad_a[0] + speed[1:2] * grad_a[1] + speed[2:3] * grad_a[2]
    thermal_current_field = padded_thermal_field[1:-1, 1:-1, 1:-1]
    grad_stack = jnp.stack(grad_t)
    new_a = a_now + 0.1 * (
        1.2 * laplace(ext_a) + carry_a - alpha * a_now - current_adjoint_vector * grad_stack
    )
    new_b = current_adjoint_vector + 0.1 * (
        1.2 * laplace(ext_b) + carry_b - 2.0 * solid * current_adjoint_vector + 2.0 * solid
    )
    common_divisor_lcm_like = jnp.sum(a_now * speed, axis=0)
    summand_contribution = (
        0.1
        * quadrature_factor
        * (
            porosity_sensitivity * common_divisor_lcm_like
            + 2.0 * (current_adjoint_vector - 1.0) * thermal_current_field
        )
    )
    return (jnp.concatenate([new_a, new_b[None]], axis=0), summand_contribution)


def halo_body(
    saved_velocity_trajectory,
    saved_warmth_trajectory,
    control_porosity,
    control_volume_flag,
    entrance_face_flag,
):
    quadrature_factor = control_volume_flag.astype(jnp.float32)
    gamma = jnp.where(control_volume_flag == 1, control_porosity, jnp.float32(0.0))
    solid = 1.0 - gamma
    alpha = 3.0 * 0.1 * solid / (0.1 + gamma)
    porosity_sensitivity = -3.0 * 0.1 * 1.1 / ((0.1 + gamma) * (0.1 + gamma))
    leading_plane = lax.axis_index("space") == 0
    trailing_plane = lax.axis_index("space") == lax.axis_size("space") - 1
    device_instant_total = saved_warmth_trajectory.shape[0]
    cycle_ext = padded(saved_warmth_trajectory, (("space", 1),), 1)

    def closing_thermal_value(thermal_current_field, with_halo_padding):
        floor_limit = jnp.where(leading_plane, thermal_current_field[0], with_halo_padding[0])
        ceiling_bound = jnp.where(trailing_plane, thermal_current_field[-1], with_halo_padding[-1])
        return pad_sides(
            jnp.concatenate(
                [floor_limit[None], thermal_current_field, ceiling_bound[None]], axis=0
            ),
            "edge",
        )

    def one_step(adj, interior_block):
        speed = saved_velocity_trajectory[interior_block].astype(jnp.float32)
        thermal_current_field = saved_warmth_trajectory[interior_block].astype(jnp.float32)
        with_halo_padding = padded(adj, (("space", 1),), 1)
        thermal_halo_values = cycle_ext[interior_block].astype(jnp.float32)
        complete_thermal_field = jnp.concatenate(
            [thermal_halo_values[:1], thermal_current_field, thermal_halo_values[-1:]], axis=0
        )
        padded_thermal_field = closing_thermal_value(thermal_current_field, complete_thermal_field)
        ext_a = pad_sides(with_halo_padding[:3], "constant")
        current_adjoint_vector = adj[3]
        floor_limit = jnp.where(
            leading_plane,
            jnp.where(entrance_face_flag == 1, jnp.float32(0.0), current_adjoint_vector[0]),
            with_halo_padding[3, 0],
        )
        ceiling_bound = jnp.where(
            trailing_plane, current_adjoint_vector[-1], with_halo_padding[3, -1]
        )
        ext_b = pad_sides(
            jnp.concatenate(
                [floor_limit[None], current_adjoint_vector, ceiling_bound[None]], axis=0
            ),
            "edge",
        )
        return adjoint_update(
            adj,
            ext_a,
            ext_b,
            padded_thermal_field,
            speed,
            alpha,
            porosity_sensitivity,
            solid,
            quadrature_factor,
        )

    grid_shape = (4,) + control_porosity.shape
    adj = jnp.zeros(grid_shape, jnp.float32)
    for interior_block in range(device_instant_total - 1, -1, -1):
        adj, unused = one_step(adj, interior_block)
    adj = passed_along(adj, "arc", -1)
    partial_sum = jnp.zeros(control_porosity.shape, jnp.float32)
    for interior_block in range(device_instant_total - 1, -1, -1):
        adj, summand_contribution = one_step(adj, interior_block)
        partial_sum = partial_sum + summand_contribution
    summed = lax.psum(partial_sum, "arc")
    share = summed.shape[1] // lax.axis_size("arc")
    gradient = lax.dynamic_slice_in_dim(summed, lax.axis_index("arc") * share, share, 1)
    return (gradient, adj[None])


def swap_over(value, partner_bit):
    count = lax.axis_size("space")
    return lax.ppermute(value, "space", [(i, i ^ partner_bit) for i in range(count)])


def in_space_order(me, axis, own, near, far, relay):
    pieces = [own, near, far, relay]
    odd = (me & 1) == 1
    pieces = [
        jnp.where(odd, pieces[1], pieces[0]),
        jnp.where(odd, pieces[0], pieces[1]),
        jnp.where(odd, pieces[3], pieces[2]),
        jnp.where(odd, pieces[2], pieces[3]),
    ]
    high = (me & 2) == 2
    pieces = [
        jnp.where(high, pieces[2], pieces[0]),
        jnp.where(high, pieces[3], pieces[1]),
        jnp.where(high, pieces[0], pieces[2]),
        jnp.where(high, pieces[1], pieces[3]),
    ]
    return jnp.concatenate(pieces, axis=axis)


def gathered_cells(local, me, axis):
    near = swap_over(local, 1)
    far = swap_over(local, 2)
    relay = swap_over(far, 1)
    return in_space_order(me, axis, local, near, far, relay)


def whole_grid_body(
    saved_velocity_trajectory,
    saved_warmth_trajectory,
    control_porosity,
    control_volume_flag,
    entrance_face_flag,
):
    lanes = saved_warmth_trajectory.shape[1]
    steps = saved_warmth_trajectory.shape[0]
    me = lax.axis_index("space")

    stacked = jnp.concatenate(
        [saved_velocity_trajectory, saved_warmth_trajectory[:, None]], axis=1
    )
    chunk = 2 if steps % 2 == 0 else 1
    tops = list(range(steps, 0, -chunk))
    near_all = swap_over(stacked, 1)
    far_chunks = [swap_over(stacked[top - chunk:top], 2) for top in tops]

    own_gamma = jnp.where(control_volume_flag == 1, control_porosity, jnp.float32(0.0))
    gamma = gathered_cells(own_gamma, me, 0)
    solid = 1.0 - gamma
    alpha = 3.0 * 0.1 * solid / (0.1 + gamma)
    own_flag = control_volume_flag.astype(jnp.float32)
    own_sensitivity = -3.0 * 0.1 * 1.1 / ((0.1 + own_gamma) * (0.1 + own_gamma))

    inputs_all = [None] * steps

    def one_step(adj, s):
        speed = inputs_all[s][:3].astype(jnp.float32)
        thermal = inputs_all[s][3].astype(jnp.float32)
        padded_thermal = jnp.pad(thermal, 1, mode="edge")
        ext_a = jnp.pad(adj[:3], ((0, 0), (1, 1), (1, 1), (1, 1)))
        b = adj[3]
        floor_limit = jnp.where(entrance_face_flag == 1, jnp.float32(0.0), b[0])
        ext_b = pad_sides(jnp.concatenate([floor_limit[None], b, b[-1][None]], axis=0), "edge")
        a_now = adj[:3]
        grad_b = slopes(ext_b)
        grad_a = slopes(ext_a)
        grad_t = slopes(padded_thermal)
        carry_b = speed[0] * grad_b[0] + speed[1] * grad_b[1] + speed[2] * grad_b[2]
        carry_a = speed[0:1] * grad_a[0] + speed[1:2] * grad_a[1] + speed[2:3] * grad_a[2]
        new_a = a_now + 0.1 * (
            1.2 * laplace(ext_a) + carry_a - alpha * a_now - b * jnp.stack(grad_t)
        )
        new_b = b + 0.1 * (1.2 * laplace(ext_b) + carry_b - 2.0 * solid * b + 2.0 * solid)
        return jnp.concatenate([new_a, new_b[None]], axis=0)

    def own_cells(x, axis):
        return lax.dynamic_slice_in_dim(x, me * lanes, lanes, axis)

    def sensitivity(adj, s):
        a_loc = own_cells(adj[:3], 1)
        b_loc = own_cells(adj[3], 0)
        speed = saved_velocity_trajectory[s].astype(jnp.float32)
        thermal = saved_warmth_trajectory[s].astype(jnp.float32)
        dot = jnp.sum(a_loc * speed, axis=0)
        return 0.1 * own_flag * (own_sensitivity * dot + 2.0 * (b_loc - 1.0) * thermal)

    grid_shape = (4,) + gamma.shape
    adj = jnp.zeros(grid_shape, jnp.float32)
    def chunk_inputs(c, far):
        relay = swap_over(far, 1)
        top = tops[c]
        for j in range(chunk):
            s = top - chunk + j
            inputs_all[s] = in_space_order(
                me, 1, stacked[s], near_all[s], far[j], relay[j]
            )

    chunk_inputs(0, far_chunks[0])
    for c, top in enumerate(tops):
        for s in range(top - 1, top - chunk - 1, -1):
            adj = one_step(adj, s)
            if s == top - 1 and c + 1 < len(tops):
                far, _ = lax.optimization_barrier((far_chunks[c + 1], adj))
                chunk_inputs(c + 1, far)

    core = me % 2
    half = adj.shape[0] // 2
    mine = lax.dynamic_slice_in_dim(adj, core * half, half, 0)
    arrived = passed_along(mine, "arc", -1)
    space_count = lax.axis_size("space")
    swap = [(i, i ^ 1) for i in range(space_count)]
    other = lax.ppermute(arrived, "space", swap)
    adj = jnp.where(
        core == 0,
        jnp.concatenate([arrived, other], axis=0),
        jnp.concatenate([other, arrived], axis=0),
    )

    partial_sum = jnp.zeros(control_porosity.shape, jnp.float32)
    for s in range(steps - 1, -1, -1):
        partial_sum = partial_sum + sensitivity(adj, s)
        adj = one_step(adj, s)

    arcs = lax.axis_size("arc")
    k = lax.axis_index("arc")
    share = partial_sum.shape[1] // arcs
    pieces = partial_sum.reshape(partial_sum.shape[0], arcs, share, partial_sum.shape[2])
    total = lax.dynamic_index_in_dim(pieces, k, 1, keepdims=False)
    for shift in range(1, arcs):
        piece = lax.dynamic_index_in_dim(pieces, (k + shift) % arcs, 1, keepdims=False)
        total = total + passed_along(piece, "arc", shift)
    entry = own_cells(adj, 1)
    return (total, entry[None])


def solution(mesh):
    chosen = whole_grid_body if mesh.shape["space"] == 4 else halo_body
    return jax.shard_map(
        chosen,
        mesh=mesh,
        in_specs=(
            P(("job", "arc"), None, "space", None, None),
            P(("job", "arc"), "space", None, None),
            P(("job", "space"), None, None),
            P(("job", "space"), None, None),
            P("job", None),
        ),
        out_specs=(P(("job", "space"), "arc", None), P(("job", "arc"), None, "space", None, None)),
        check_vma=False,
    )
```

```python
import jax
import jax.numpy as jnp
from jax import lax
from jax.sharding import PartitionSpec as P


def padded(cells, sides, width):
    for axis, dim in sides:
        count = lax.axis_size(axis)
        ends = count - 1
        head = lax.slice_in_dim(cells, 0, width, axis=dim)
        tail = lax.slice_in_dim(cells, cells.shape[dim] - width, cells.shape[dim], axis=dim)
        cells = jnp.concatenate(
            [
                lax.ppermute(tail, axis, [(i, (i + 1) % count) for i in range(ends)]),
                cells,
                lax.ppermute(head, axis, [((i + 1) % count, i) for i in range(ends)]),
            ],
            axis=dim,
        )
    return cells


def passed_along(value, axis, steps):
    count = lax.axis_size(axis)
    pairs = [(source, (source + steps) % count) for source in range(count)]
    return lax.ppermute(value, axis, pairs)


def laplace(ext):
    mid = ext[..., 1:-1, 1:-1, 1:-1]
    total = ext[..., 2:, 1:-1, 1:-1] + ext[..., :-2, 1:-1, 1:-1]
    total = total + ext[..., 1:-1, 2:, 1:-1] + ext[..., 1:-1, :-2, 1:-1]
    total = total + ext[..., 1:-1, 1:-1, 2:] + ext[..., 1:-1, 1:-1, :-2]
    return total - 6.0 * mid


def slopes(ext):
    return (
        0.5 * (ext[..., 2:, 1:-1, 1:-1] - ext[..., :-2, 1:-1, 1:-1]),
        0.5 * (ext[..., 1:-1, 2:, 1:-1] - ext[..., 1:-1, :-2, 1:-1]),
        0.5 * (ext[..., 1:-1, 1:-1, 2:] - ext[..., 1:-1, 1:-1, :-2]),
    )


def pad_sides(field, operating_variant):
    widths = [(0, 0)] * (field.ndim - 2) + [(1, 1), (1, 1)]
    return jnp.pad(field, widths, mode=operating_variant)


def adjoint_update(
    adj,
    ext_a,
    ext_b,
    padded_thermal_field,
    speed,
    alpha,
    porosity_sensitivity,
    solid,
    quadrature_factor,
):
    a_now = adj[:3]
    current_adjoint_vector = adj[3]
    grad_b = slopes(ext_b)
    grad_a = slopes(ext_a)
    grad_t = slopes(padded_thermal_field)
    carry_b = speed[0] * grad_b[0] + speed[1] * grad_b[1] + speed[2] * grad_b[2]
    carry_a = speed[0:1] * grad_a[0] + speed[1:2] * grad_a[1] + speed[2:3] * grad_a[2]
    thermal_current_field = padded_thermal_field[1:-1, 1:-1, 1:-1]
    grad_stack = jnp.stack(grad_t)
    new_a = a_now + 0.1 * (
        1.2 * laplace(ext_a) + carry_a - alpha * a_now - current_adjoint_vector * grad_stack
    )
    new_b = current_adjoint_vector + 0.1 * (
        1.2 * laplace(ext_b) + carry_b - 2.0 * solid * current_adjoint_vector + 2.0 * solid
    )
    common_divisor_lcm_like = jnp.sum(a_now * speed, axis=0)
    summand_contribution = (
        0.1
        * quadrature_factor
        * (
            porosity_sensitivity * common_divisor_lcm_like
            + 2.0 * (current_adjoint_vector - 1.0) * thermal_current_field
        )
    )
    return (jnp.concatenate([new_a, new_b[None]], axis=0), summand_contribution)


def halo_body(
    saved_velocity_trajectory,
    saved_warmth_trajectory,
    control_porosity,
    control_volume_flag,
    entrance_face_flag,
):
    quadrature_factor = control_volume_flag.astype(jnp.float32)
    gamma = jnp.where(control_volume_flag == 1, control_porosity, jnp.float32(0.0))
    solid = 1.0 - gamma
    alpha = 3.0 * 0.1 * solid / (0.1 + gamma)
    porosity_sensitivity = -3.0 * 0.1 * 1.1 / ((0.1 + gamma) * (0.1 + gamma))
    leading_plane = lax.axis_index("space") == 0
    trailing_plane = lax.axis_index("space") == lax.axis_size("space") - 1
    device_instant_total = saved_warmth_trajectory.shape[0]
    cycle_ext = padded(saved_warmth_trajectory, (("space", 1),), 1)

    def closing_thermal_value(thermal_current_field, with_halo_padding):
        floor_limit = jnp.where(leading_plane, thermal_current_field[0], with_halo_padding[0])
        ceiling_bound = jnp.where(trailing_plane, thermal_current_field[-1], with_halo_padding[-1])
        return pad_sides(
            jnp.concatenate(
                [floor_limit[None], thermal_current_field, ceiling_bound[None]], axis=0
            ),
            "edge",
        )

    def one_step(adj, interior_block):
        speed = saved_velocity_trajectory[interior_block].astype(jnp.float32)
        thermal_current_field = saved_warmth_trajectory[interior_block].astype(jnp.float32)
        with_halo_padding = padded(adj, (("space", 1),), 1)
        thermal_halo_values = cycle_ext[interior_block].astype(jnp.float32)
        complete_thermal_field = jnp.concatenate(
            [thermal_halo_values[:1], thermal_current_field, thermal_halo_values[-1:]], axis=0
        )
        padded_thermal_field = closing_thermal_value(thermal_current_field, complete_thermal_field)
        ext_a = pad_sides(with_halo_padding[:3], "constant")
        current_adjoint_vector = adj[3]
        floor_limit = jnp.where(
            leading_plane,
            jnp.where(entrance_face_flag == 1, jnp.float32(0.0), current_adjoint_vector[0]),
            with_halo_padding[3, 0],
        )
        ceiling_bound = jnp.where(
            trailing_plane, current_adjoint_vector[-1], with_halo_padding[3, -1]
        )
        ext_b = pad_sides(
            jnp.concatenate(
                [floor_limit[None], current_adjoint_vector, ceiling_bound[None]], axis=0
            ),
            "edge",
        )
        return adjoint_update(
            adj,
            ext_a,
            ext_b,
            padded_thermal_field,
            speed,
            alpha,
            porosity_sensitivity,
            solid,
            quadrature_factor,
        )

    grid_shape = (4,) + control_porosity.shape
    adj = jnp.zeros(grid_shape, jnp.float32)
    for interior_block in range(device_instant_total - 1, -1, -1):
        adj, unused = one_step(adj, interior_block)
    adj = passed_along(adj, "arc", -1)
    partial_sum = jnp.zeros(control_porosity.shape, jnp.float32)
    for interior_block in range(device_instant_total - 1, -1, -1):
        adj, summand_contribution = one_step(adj, interior_block)
        partial_sum = partial_sum + summand_contribution
    summed = lax.psum(partial_sum, "arc")
    share = summed.shape[1] // lax.axis_size("arc")
    gradient = lax.dynamic_slice_in_dim(summed, lax.axis_index("arc") * share, share, 1)
    return (gradient, adj[None])


def swap_over(value, partner_bit):
    count = lax.axis_size("space")
    return lax.ppermute(value, "space", [(i, i ^ partner_bit) for i in range(count)])


def in_space_order(me, axis, own, near, far, relay):
    pieces = [own, near, far, relay]
    odd = (me & 1) == 1
    pieces = [
        jnp.where(odd, pieces[1], pieces[0]),
        jnp.where(odd, pieces[0], pieces[1]),
        jnp.where(odd, pieces[3], pieces[2]),
        jnp.where(odd, pieces[2], pieces[3]),
    ]
    high = (me & 2) == 2
    pieces = [
        jnp.where(high, pieces[2], pieces[0]),
        jnp.where(high, pieces[3], pieces[1]),
        jnp.where(high, pieces[0], pieces[2]),
        jnp.where(high, pieces[1], pieces[3]),
    ]
    return jnp.concatenate(pieces, axis=axis)


def gathered_cells(local, me, axis):
    near = swap_over(local, 1)
    far = swap_over(local, 2)
    relay = swap_over(far, 1)
    return in_space_order(me, axis, local, near, far, relay)


def whole_grid_body(
    saved_velocity_trajectory,
    saved_warmth_trajectory,
    control_porosity,
    control_volume_flag,
    entrance_face_flag,
):
    lanes = saved_warmth_trajectory.shape[1]
    steps = saved_warmth_trajectory.shape[0]
    me = lax.axis_index("space")

    stacked = jnp.concatenate(
        [saved_velocity_trajectory, saved_warmth_trajectory[:, None]], axis=1
    )
    chunk = 2 if steps % 2 == 0 else 1
    tops = list(range(steps, 0, -chunk))
    near_all = swap_over(stacked, 1)
    lead = 2
    far_chunks = [swap_over(stacked[top - chunk:top], 2) for top in tops[:lead]]

    own_gamma = jnp.where(control_volume_flag == 1, control_porosity, jnp.float32(0.0))
    gamma = gathered_cells(own_gamma, me, 0)
    solid = 1.0 - gamma
    alpha = 3.0 * 0.1 * solid / (0.1 + gamma)
    own_flag = control_volume_flag.astype(jnp.float32)
    own_sensitivity = -3.0 * 0.1 * 1.1 / ((0.1 + own_gamma) * (0.1 + own_gamma))

    inputs_all = [None] * steps

    def one_step(adj, s):
        speed = inputs_all[s][:3].astype(jnp.float32)
        thermal = inputs_all[s][3].astype(jnp.float32)
        padded_thermal = jnp.pad(thermal, 1, mode="edge")
        ext_a = jnp.pad(adj[:3], ((0, 0), (1, 1), (1, 1), (1, 1)))
        b = adj[3]
        floor_limit = jnp.where(entrance_face_flag == 1, jnp.float32(0.0), b[0])
        ext_b = pad_sides(jnp.concatenate([floor_limit[None], b, b[-1][None]], axis=0), "edge")
        a_now = adj[:3]
        grad_b = slopes(ext_b)
        grad_a = slopes(ext_a)
        grad_t = slopes(padded_thermal)
        carry_b = speed[0] * grad_b[0] + speed[1] * grad_b[1] + speed[2] * grad_b[2]
        carry_a = speed[0:1] * grad_a[0] + speed[1:2] * grad_a[1] + speed[2:3] * grad_a[2]
        new_a = a_now + 0.1 * (
            1.2 * laplace(ext_a) + carry_a - alpha * a_now - b * jnp.stack(grad_t)
        )
        new_b = b + 0.1 * (1.2 * laplace(ext_b) + carry_b - 2.0 * solid * b + 2.0 * solid)
        return jnp.concatenate([new_a, new_b[None]], axis=0)

    def own_cells(x, axis):
        return lax.dynamic_slice_in_dim(x, me * lanes, lanes, axis)

    def sensitivity(adj, s):
        a_loc = own_cells(adj[:3], 1)
        b_loc = own_cells(adj[3], 0)
        speed = saved_velocity_trajectory[s].astype(jnp.float32)
        thermal = saved_warmth_trajectory[s].astype(jnp.float32)
        dot = jnp.sum(a_loc * speed, axis=0)
        return 0.1 * own_flag * (own_sensitivity * dot + 2.0 * (b_loc - 1.0) * thermal)

    grid_shape = (4,) + gamma.shape
    adj = jnp.zeros(grid_shape, jnp.float32)
    def chunk_inputs(c, far):
        relay = swap_over(far, 1)
        top = tops[c]
        for j in range(chunk):
            s = top - chunk + j
            inputs_all[s] = in_space_order(
                me, 1, stacked[s], near_all[s], far[j], relay[j]
            )

    chunk_inputs(0, far_chunks[0])
    for c, top in enumerate(tops):
        for s in range(top - 1, top - chunk - 1, -1):
            adj = one_step(adj, s)
            if s == top - 1 and c + lead < len(tops):
                later = tops[c + lead]
                anchor = jnp.float32(0.0) * adj[0, 0, 0, 0]
                held = (stacked[later - chunk:later].astype(jnp.float32) + anchor).astype(
                    stacked.dtype
                )
                far_chunks.append(swap_over(held, 2))
        if c + 1 < len(tops):
            chunk_inputs(c + 1, far_chunks[c + 1])

    core = me % 2
    half = adj.shape[0] // 2
    mine = lax.dynamic_slice_in_dim(adj, core * half, half, 0)
    arrived = passed_along(mine, "arc", -1)
    space_count = lax.axis_size("space")
    swap = [(i, i ^ 1) for i in range(space_count)]
    other = lax.ppermute(arrived, "space", swap)
    adj = jnp.where(
        core == 0,
        jnp.concatenate([arrived, other], axis=0),
        jnp.concatenate([other, arrived], axis=0),
    )

    partial_sum = jnp.zeros(control_porosity.shape, jnp.float32)
    for s in range(steps - 1, -1, -1):
        partial_sum = partial_sum + sensitivity(adj, s)
        adj = one_step(adj, s)

    arcs = lax.axis_size("arc")
    k = lax.axis_index("arc")
    share = partial_sum.shape[1] // arcs
    pieces = partial_sum.reshape(partial_sum.shape[0], arcs, share, partial_sum.shape[2])
    total = lax.dynamic_index_in_dim(pieces, k, 1, keepdims=False)
    for shift in range(1, arcs):
        piece = lax.dynamic_index_in_dim(pieces, (k + shift) % arcs, 1, keepdims=False)
        total = total + passed_along(piece, "arc", shift)
    entry = own_cells(adj, 1)
    return (total, entry[None])


def solution(mesh):
    chosen = whole_grid_body if mesh.shape["space"] == 4 else halo_body
    return jax.shard_map(
        chosen,
        mesh=mesh,
        in_specs=(
            P(("job", "arc"), None, "space", None, None),
            P(("job", "arc"), "space", None, None),
            P(("job", "space"), None, None),
            P(("job", "space"), None, None),
            P("job", None),
        ),
        out_specs=(P(("job", "space"), "arc", None), P(("job", "arc"), None, "space", None, None)),
        check_vma=False,
    )
```

```python
import jax
import jax.numpy as jnp
from jax import lax
from jax.sharding import PartitionSpec as P


def padded(cells, sides, width):
    for axis, dim in sides:
        count = lax.axis_size(axis)
        ends = count - 1
        head = lax.slice_in_dim(cells, 0, width, axis=dim)
        tail = lax.slice_in_dim(cells, cells.shape[dim] - width, cells.shape[dim], axis=dim)
        cells = jnp.concatenate(
            [
                lax.ppermute(tail, axis, [(i, (i + 1) % count) for i in range(ends)]),
                cells,
                lax.ppermute(head, axis, [((i + 1) % count, i) for i in range(ends)]),
            ],
            axis=dim,
        )
    return cells


def passed_along(value, axis, steps):
    count = lax.axis_size(axis)
    pairs = [(source, (source + steps) % count) for source in range(count)]
    return lax.ppermute(value, axis, pairs)


def laplace(ext):
    mid = ext[..., 1:-1, 1:-1, 1:-1]
    total = ext[..., 2:, 1:-1, 1:-1] + ext[..., :-2, 1:-1, 1:-1]
    total = total + ext[..., 1:-1, 2:, 1:-1] + ext[..., 1:-1, :-2, 1:-1]
    total = total + ext[..., 1:-1, 1:-1, 2:] + ext[..., 1:-1, 1:-1, :-2]
    return total - 6.0 * mid


def slopes(ext):
    return (
        0.5 * (ext[..., 2:, 1:-1, 1:-1] - ext[..., :-2, 1:-1, 1:-1]),
        0.5 * (ext[..., 1:-1, 2:, 1:-1] - ext[..., 1:-1, :-2, 1:-1]),
        0.5 * (ext[..., 1:-1, 1:-1, 2:] - ext[..., 1:-1, 1:-1, :-2]),
    )


def pad_sides(field, operating_variant):
    widths = [(0, 0)] * (field.ndim - 2) + [(1, 1), (1, 1)]
    return jnp.pad(field, widths, mode=operating_variant)


def adjoint_update(
    adj,
    ext_a,
    ext_b,
    padded_thermal_field,
    speed,
    alpha,
    porosity_sensitivity,
    solid,
    quadrature_factor,
):
    a_now = adj[:3]
    current_adjoint_vector = adj[3]
    grad_b = slopes(ext_b)
    grad_a = slopes(ext_a)
    grad_t = slopes(padded_thermal_field)
    carry_b = speed[0] * grad_b[0] + speed[1] * grad_b[1] + speed[2] * grad_b[2]
    carry_a = speed[0:1] * grad_a[0] + speed[1:2] * grad_a[1] + speed[2:3] * grad_a[2]
    thermal_current_field = padded_thermal_field[1:-1, 1:-1, 1:-1]
    grad_stack = jnp.stack(grad_t)
    new_a = a_now + 0.1 * (
        1.2 * laplace(ext_a) + carry_a - alpha * a_now - current_adjoint_vector * grad_stack
    )
    new_b = current_adjoint_vector + 0.1 * (
        1.2 * laplace(ext_b) + carry_b - 2.0 * solid * current_adjoint_vector + 2.0 * solid
    )
    common_divisor_lcm_like = jnp.sum(a_now * speed, axis=0)
    summand_contribution = (
        0.1
        * quadrature_factor
        * (
            porosity_sensitivity * common_divisor_lcm_like
            + 2.0 * (current_adjoint_vector - 1.0) * thermal_current_field
        )
    )
    return (jnp.concatenate([new_a, new_b[None]], axis=0), summand_contribution)


def halo_body(
    saved_velocity_trajectory,
    saved_warmth_trajectory,
    control_porosity,
    control_volume_flag,
    entrance_face_flag,
):
    quadrature_factor = control_volume_flag.astype(jnp.float32)
    gamma = jnp.where(control_volume_flag == 1, control_porosity, jnp.float32(0.0))
    solid = 1.0 - gamma
    alpha = 3.0 * 0.1 * solid / (0.1 + gamma)
    porosity_sensitivity = -3.0 * 0.1 * 1.1 / ((0.1 + gamma) * (0.1 + gamma))
    leading_plane = lax.axis_index("space") == 0
    trailing_plane = lax.axis_index("space") == lax.axis_size("space") - 1
    device_instant_total = saved_warmth_trajectory.shape[0]
    cycle_ext = padded(saved_warmth_trajectory, (("space", 1),), 1)

    def closing_thermal_value(thermal_current_field, with_halo_padding):
        floor_limit = jnp.where(leading_plane, thermal_current_field[0], with_halo_padding[0])
        ceiling_bound = jnp.where(trailing_plane, thermal_current_field[-1], with_halo_padding[-1])
        return pad_sides(
            jnp.concatenate(
                [floor_limit[None], thermal_current_field, ceiling_bound[None]], axis=0
            ),
            "edge",
        )

    def one_step(adj, interior_block):
        speed = saved_velocity_trajectory[interior_block].astype(jnp.float32)
        thermal_current_field = saved_warmth_trajectory[interior_block].astype(jnp.float32)
        with_halo_padding = padded(adj, (("space", 1),), 1)
        thermal_halo_values = cycle_ext[interior_block].astype(jnp.float32)
        complete_thermal_field = jnp.concatenate(
            [thermal_halo_values[:1], thermal_current_field, thermal_halo_values[-1:]], axis=0
        )
        padded_thermal_field = closing_thermal_value(thermal_current_field, complete_thermal_field)
        ext_a = pad_sides(with_halo_padding[:3], "constant")
        current_adjoint_vector = adj[3]
        floor_limit = jnp.where(
            leading_plane,
            jnp.where(entrance_face_flag == 1, jnp.float32(0.0), current_adjoint_vector[0]),
            with_halo_padding[3, 0],
        )
        ceiling_bound = jnp.where(
            trailing_plane, current_adjoint_vector[-1], with_halo_padding[3, -1]
        )
        ext_b = pad_sides(
            jnp.concatenate(
                [floor_limit[None], current_adjoint_vector, ceiling_bound[None]], axis=0
            ),
            "edge",
        )
        return adjoint_update(
            adj,
            ext_a,
            ext_b,
            padded_thermal_field,
            speed,
            alpha,
            porosity_sensitivity,
            solid,
            quadrature_factor,
        )

    grid_shape = (4,) + control_porosity.shape
    adj = jnp.zeros(grid_shape, jnp.float32)
    for interior_block in range(device_instant_total - 1, -1, -1):
        adj, unused = one_step(adj, interior_block)
    adj = passed_along(adj, "arc", -1)
    partial_sum = jnp.zeros(control_porosity.shape, jnp.float32)
    for interior_block in range(device_instant_total - 1, -1, -1):
        adj, summand_contribution = one_step(adj, interior_block)
        partial_sum = partial_sum + summand_contribution
    summed = lax.psum(partial_sum, "arc")
    share = summed.shape[1] // lax.axis_size("arc")
    gradient = lax.dynamic_slice_in_dim(summed, lax.axis_index("arc") * share, share, 1)
    return (gradient, adj[None])


def swap_over(value, partner_bit):
    count = lax.axis_size("space")
    return lax.ppermute(value, "space", [(i, i ^ partner_bit) for i in range(count)])


def in_space_order(me, axis, own, near, far, relay):
    pieces = [own, near, far, relay]
    odd = (me & 1) == 1
    pieces = [
        jnp.where(odd, pieces[1], pieces[0]),
        jnp.where(odd, pieces[0], pieces[1]),
        jnp.where(odd, pieces[3], pieces[2]),
        jnp.where(odd, pieces[2], pieces[3]),
    ]
    high = (me & 2) == 2
    pieces = [
        jnp.where(high, pieces[2], pieces[0]),
        jnp.where(high, pieces[3], pieces[1]),
        jnp.where(high, pieces[0], pieces[2]),
        jnp.where(high, pieces[1], pieces[3]),
    ]
    return jnp.concatenate(pieces, axis=axis)


def gathered_cells(local, me, axis):
    near = swap_over(local, 1)
    far = swap_over(local, 2)
    relay = swap_over(far, 1)
    return in_space_order(me, axis, local, near, far, relay)


def whole_grid_body(
    saved_velocity_trajectory,
    saved_warmth_trajectory,
    control_porosity,
    control_volume_flag,
    entrance_face_flag,
):
    lanes = saved_warmth_trajectory.shape[1]
    steps = saved_warmth_trajectory.shape[0]
    me = lax.axis_index("space")

    stacked = jnp.concatenate(
        [saved_velocity_trajectory, saved_warmth_trajectory[:, None]], axis=1
    )
    inputs_all = [None] * steps
    chunk = 2 if steps % 2 == 0 else 1
    near_all = swap_over(stacked, 1)
    for top in range(steps, 0, -chunk):
        own = stacked[top - chunk:top]
        far = swap_over(own, 2)
        relay = swap_over(far, 1)
        piece = in_space_order(me, 2, own, near_all[top - chunk:top], far, relay)
        for j in range(chunk):
            inputs_all[top - chunk + j] = piece[j]

    own_gamma = jnp.where(control_volume_flag == 1, control_porosity, jnp.float32(0.0))
    gamma = gathered_cells(own_gamma, me, 0)
    solid = 1.0 - gamma
    alpha = 3.0 * 0.1 * solid / (0.1 + gamma)
    own_flag = control_volume_flag.astype(jnp.float32)
    own_sensitivity = -3.0 * 0.1 * 1.1 / ((0.1 + own_gamma) * (0.1 + own_gamma))

    def one_step(adj, s):
        speed = inputs_all[s][:3].astype(jnp.float32)
        thermal = inputs_all[s][3].astype(jnp.float32)
        padded_thermal = jnp.pad(thermal, 1, mode="edge")
        ext_a = jnp.pad(adj[:3], ((0, 0), (1, 1), (1, 1), (1, 1)))
        b = adj[3]
        floor_limit = jnp.where(entrance_face_flag == 1, jnp.float32(0.0), b[0])
        ext_b = pad_sides(jnp.concatenate([floor_limit[None], b, b[-1][None]], axis=0), "edge")
        a_now = adj[:3]
        grad_b = slopes(ext_b)
        grad_a = slopes(ext_a)
        grad_t = slopes(padded_thermal)
        carry_b = speed[0] * grad_b[0] + speed[1] * grad_b[1] + speed[2] * grad_b[2]
        carry_a = speed[0:1] * grad_a[0] + speed[1:2] * grad_a[1] + speed[2:3] * grad_a[2]
        new_a = a_now + 0.1 * (
            1.2 * laplace(ext_a) + carry_a - alpha * a_now - b * jnp.stack(grad_t)
        )
        new_b = b + 0.1 * (1.2 * laplace(ext_b) + carry_b - 2.0 * solid * b + 2.0 * solid)
        return jnp.concatenate([new_a, new_b[None]], axis=0)

    def own_cells(x, axis):
        return lax.dynamic_slice_in_dim(x, me * lanes, lanes, axis)

    def sensitivity(adj, s):
        a_loc = own_cells(adj[:3], 1)
        b_loc = own_cells(adj[3], 0)
        speed = saved_velocity_trajectory[s].astype(jnp.float32)
        thermal = saved_warmth_trajectory[s].astype(jnp.float32)
        dot = jnp.sum(a_loc * speed, axis=0)
        return 0.1 * own_flag * (own_sensitivity * dot + 2.0 * (b_loc - 1.0) * thermal)

    grid_shape = (4,) + gamma.shape
    adj = jnp.zeros(grid_shape, jnp.float32)
    for s in range(steps - 1, -1, -1):
        adj = one_step(adj, s)

    core = me % 2
    half = adj.shape[0] // 2
    mine = lax.dynamic_slice_in_dim(adj, core * half, half, 0)
    arrived = passed_along(mine, "arc", -1)
    space_count = lax.axis_size("space")
    swap = [(i, i ^ 1) for i in range(space_count)]
    other = lax.ppermute(arrived, "space", swap)
    adj = jnp.where(
        core == 0,
        jnp.concatenate([arrived, other], axis=0),
        jnp.concatenate([other, arrived], axis=0),
    )

    partial_sum = jnp.zeros(control_porosity.shape, jnp.float32)
    for s in range(steps - 1, -1, -1):
        partial_sum = partial_sum + sensitivity(adj, s)
        adj = one_step(adj, s)

    arcs = lax.axis_size("arc")
    k = lax.axis_index("arc")
    share = partial_sum.shape[1] // arcs
    pieces = partial_sum.reshape(partial_sum.shape[0], arcs, share, partial_sum.shape[2])
    total = lax.dynamic_index_in_dim(pieces, k, 1, keepdims=False)
    for shift in range(1, arcs):
        piece = lax.dynamic_index_in_dim(pieces, (k + shift) % arcs, 1, keepdims=False)
        total = total + passed_along(piece, "arc", shift)
    entry = own_cells(adj, 1)
    return (total, entry[None])


def solution(mesh):
    chosen = whole_grid_body if mesh.shape["space"] == 4 else halo_body
    return jax.shard_map(
        chosen,
        mesh=mesh,
        in_specs=(
            P(("job", "arc"), None, "space", None, None),
            P(("job", "arc"), "space", None, None),
            P(("job", "space"), None, None),
            P(("job", "space"), None, None),
            P("job", None),
        ),
        out_specs=(P(("job", "space"), "arc", None), P(("job", "arc"), None, "space", None, None)),
        check_vma=False,
    )
```

```python
import jax
import jax.numpy as jnp
from jax import lax
from jax.experimental import pallas as pl
from jax.experimental.pallas import tpu as pltpu
from jax.sharding import PartitionSpec as P


def padded(cells, sides, width):
    for axis, dim in sides:
        count = lax.axis_size(axis)
        ends = count - 1
        head = lax.slice_in_dim(cells, 0, width, axis=dim)
        tail = lax.slice_in_dim(cells, cells.shape[dim] - width, cells.shape[dim], axis=dim)
        cells = jnp.concatenate(
            [
                lax.ppermute(tail, axis, [(i, (i + 1) % count) for i in range(ends)]),
                cells,
                lax.ppermute(head, axis, [((i + 1) % count, i) for i in range(ends)]),
            ],
            axis=dim,
        )
    return cells


def passed_along(value, axis, steps):
    count = lax.axis_size(axis)
    pairs = [(source, (source + steps) % count) for source in range(count)]
    return lax.ppermute(value, axis, pairs)


def laplace(ext):
    mid = ext[..., 1:-1, 1:-1, 1:-1]
    total = ext[..., 2:, 1:-1, 1:-1] + ext[..., :-2, 1:-1, 1:-1]
    total = total + ext[..., 1:-1, 2:, 1:-1] + ext[..., 1:-1, :-2, 1:-1]
    total = total + ext[..., 1:-1, 1:-1, 2:] + ext[..., 1:-1, 1:-1, :-2]
    return total - 6.0 * mid


def slopes(ext):
    return (
        0.5 * (ext[..., 2:, 1:-1, 1:-1] - ext[..., :-2, 1:-1, 1:-1]),
        0.5 * (ext[..., 1:-1, 2:, 1:-1] - ext[..., 1:-1, :-2, 1:-1]),
        0.5 * (ext[..., 1:-1, 1:-1, 2:] - ext[..., 1:-1, 1:-1, :-2]),
    )


def pad_sides(field, operating_variant):
    widths = [(0, 0)] * (field.ndim - 2) + [(1, 1), (1, 1)]
    return jnp.pad(field, widths, mode=operating_variant)


def adjoint_update(
    adj,
    ext_a,
    ext_b,
    padded_thermal_field,
    speed,
    alpha,
    porosity_sensitivity,
    solid,
    quadrature_factor,
):
    a_now = adj[:3]
    current_adjoint_vector = adj[3]
    grad_b = slopes(ext_b)
    grad_a = slopes(ext_a)
    grad_t = slopes(padded_thermal_field)
    carry_b = speed[0] * grad_b[0] + speed[1] * grad_b[1] + speed[2] * grad_b[2]
    carry_a = speed[0:1] * grad_a[0] + speed[1:2] * grad_a[1] + speed[2:3] * grad_a[2]
    thermal_current_field = padded_thermal_field[1:-1, 1:-1, 1:-1]
    grad_stack = jnp.stack(grad_t)
    new_a = a_now + 0.1 * (
        1.2 * laplace(ext_a) + carry_a - alpha * a_now - current_adjoint_vector * grad_stack
    )
    new_b = current_adjoint_vector + 0.1 * (
        1.2 * laplace(ext_b) + carry_b - 2.0 * solid * current_adjoint_vector + 2.0 * solid
    )
    common_divisor_lcm_like = jnp.sum(a_now * speed, axis=0)
    summand_contribution = (
        0.1
        * quadrature_factor
        * (
            porosity_sensitivity * common_divisor_lcm_like
            + 2.0 * (current_adjoint_vector - 1.0) * thermal_current_field
        )
    )
    return (jnp.concatenate([new_a, new_b[None]], axis=0), summand_contribution)


def halo_body(
    saved_velocity_trajectory,
    saved_warmth_trajectory,
    control_porosity,
    control_volume_flag,
    entrance_face_flag,
):
    quadrature_factor = control_volume_flag.astype(jnp.float32)
    gamma = jnp.where(control_volume_flag == 1, control_porosity, jnp.float32(0.0))
    solid = 1.0 - gamma
    alpha = 3.0 * 0.1 * solid / (0.1 + gamma)
    porosity_sensitivity = -3.0 * 0.1 * 1.1 / ((0.1 + gamma) * (0.1 + gamma))
    leading_plane = lax.axis_index("space") == 0
    trailing_plane = lax.axis_index("space") == lax.axis_size("space") - 1
    device_instant_total = saved_warmth_trajectory.shape[0]
    cycle_ext = padded(saved_warmth_trajectory, (("space", 1),), 1)

    def closing_thermal_value(thermal_current_field, with_halo_padding):
        floor_limit = jnp.where(leading_plane, thermal_current_field[0], with_halo_padding[0])
        ceiling_bound = jnp.where(trailing_plane, thermal_current_field[-1], with_halo_padding[-1])
        return pad_sides(
            jnp.concatenate(
                [floor_limit[None], thermal_current_field, ceiling_bound[None]], axis=0
            ),
            "edge",
        )

    def one_step(adj, interior_block):
        speed = saved_velocity_trajectory[interior_block].astype(jnp.float32)
        thermal_current_field = saved_warmth_trajectory[interior_block].astype(jnp.float32)
        with_halo_padding = padded(adj, (("space", 1),), 1)
        thermal_halo_values = cycle_ext[interior_block].astype(jnp.float32)
        complete_thermal_field = jnp.concatenate(
            [thermal_halo_values[:1], thermal_current_field, thermal_halo_values[-1:]], axis=0
        )
        padded_thermal_field = closing_thermal_value(thermal_current_field, complete_thermal_field)
        ext_a = pad_sides(with_halo_padding[:3], "constant")
        current_adjoint_vector = adj[3]
        floor_limit = jnp.where(
            leading_plane,
            jnp.where(entrance_face_flag == 1, jnp.float32(0.0), current_adjoint_vector[0]),
            with_halo_padding[3, 0],
        )
        ceiling_bound = jnp.where(
            trailing_plane, current_adjoint_vector[-1], with_halo_padding[3, -1]
        )
        ext_b = pad_sides(
            jnp.concatenate(
                [floor_limit[None], current_adjoint_vector, ceiling_bound[None]], axis=0
            ),
            "edge",
        )
        return adjoint_update(
            adj,
            ext_a,
            ext_b,
            padded_thermal_field,
            speed,
            alpha,
            porosity_sensitivity,
            solid,
            quadrature_factor,
        )

    grid_shape = (4,) + control_porosity.shape
    adj = jnp.zeros(grid_shape, jnp.float32)
    for interior_block in range(device_instant_total - 1, -1, -1):
        adj, unused = one_step(adj, interior_block)
    adj = passed_along(adj, "arc", -1)
    partial_sum = jnp.zeros(control_porosity.shape, jnp.float32)
    for interior_block in range(device_instant_total - 1, -1, -1):
        adj, summand_contribution = one_step(adj, interior_block)
        partial_sum = partial_sum + summand_contribution
    summed = lax.psum(partial_sum, "arc")
    share = summed.shape[1] // lax.axis_size("arc")
    gradient = lax.dynamic_slice_in_dim(summed, lax.axis_index("arc") * share, share, 1)
    return (gradient, adj[None])


def swap_over(value, partner_bit):
    count = lax.axis_size("space")
    return lax.ppermute(value, "space", [(i, i ^ partner_bit) for i in range(count)])


def in_space_order(me, axis, own, near, far, relay):
    pieces = [own, near, far, relay]
    odd = (me & 1) == 1
    pieces = [
        jnp.where(odd, pieces[1], pieces[0]),
        jnp.where(odd, pieces[0], pieces[1]),
        jnp.where(odd, pieces[3], pieces[2]),
        jnp.where(odd, pieces[2], pieces[3]),
    ]
    high = (me & 2) == 2
    pieces = [
        jnp.where(high, pieces[2], pieces[0]),
        jnp.where(high, pieces[3], pieces[1]),
        jnp.where(high, pieces[0], pieces[2]),
        jnp.where(high, pieces[1], pieces[3]),
    ]
    return jnp.concatenate(pieces, axis=axis)


def gathered_cells(local, me, axis):
    near = swap_over(local, 1)
    far = swap_over(local, 2)
    relay = swap_over(far, 1)
    return in_space_order(me, axis, local, near, far, relay)


def _shifted(f, axis, edge):
    n = f.shape[axis]
    idx = lax.broadcasted_iota(jnp.int32, f.shape, axis)
    up = pltpu.roll(f, n - 1, axis)
    down = pltpu.roll(f, 1, axis)
    up = jnp.where(idx == n - 1, f if edge else 0.0, up)
    down = jnp.where(idx == 0, f if edge else 0.0, down)
    return up, down


def _step_kernel(adj_ref, inp_ref, alpha_ref, solid_ref, ent_ref, out_ref):
    cells = adj_ref.shape[1]
    floor = ent_ref[...]
    for i in range(cells):
        lo = max(i - 1, 0)
        hi = min(i + 1, cells - 1)
        u = [inp_ref[d, i].astype(jnp.float32) for d in range(3)]
        t = inp_ref[3, i].astype(jnp.float32)
        t_hi = inp_ref[3, hi].astype(jnp.float32)
        t_lo = inp_ref[3, lo].astype(jnp.float32)
        t_r = _shifted(t, 0, True)
        t_l = _shifted(t, 1, True)
        grad_t = (0.5 * (t_hi - t_lo), 0.5 * (t_r[0] - t_r[1]), 0.5 * (t_l[0] - t_l[1]))
        b = adj_ref[3, i]
        b_hi = adj_ref[3, hi]
        if i == 0:
            b_lo = jnp.where(floor == 1.0, 0.0, b)
        else:
            b_lo = adj_ref[3, lo]
        alpha = alpha_ref[i]
        solid = solid_ref[i]
        for c in range(3):
            a = adj_ref[c, i]
            a_hi = adj_ref[c, hi] if i + 1 < cells else jnp.zeros_like(a)
            a_lo = adj_ref[c, lo] if i > 0 else jnp.zeros_like(a)
            a_r = _shifted(a, 0, False)
            a_l = _shifted(a, 1, False)
            lap = (a_hi + a_lo) + a_r[0] + a_r[1] + a_l[0] + a_l[1] - 6.0 * a
            carry = (
                u[0] * (0.5 * (a_hi - a_lo))
                + u[1] * (0.5 * (a_r[0] - a_r[1]))
                + u[2] * (0.5 * (a_l[0] - a_l[1]))
            )
            out_ref[c, i] = a + 0.1 * (1.2 * lap + carry - alpha * a - b * grad_t[c])
        b_r = _shifted(b, 0, True)
        b_l = _shifted(b, 1, True)
        lap_b = (b_hi + b_lo) + b_r[0] + b_r[1] + b_l[0] + b_l[1] - 6.0 * b
        carry_b = (
            u[0] * (0.5 * (b_hi - b_lo))
            + u[1] * (0.5 * (b_r[0] - b_r[1]))
            + u[2] * (0.5 * (b_l[0] - b_l[1]))
        )
        out_ref[3, i] = b + 0.1 * (1.2 * lap_b + carry_b - 2.0 * solid * b + 2.0 * solid)


def kernel_step(adj, inputs, alpha, solid, floor):
    vmem = pl.BlockSpec(memory_space=pltpu.VMEM)
    n = adj.size
    return pl.pallas_call(
        _step_kernel,
        out_shape=jax.ShapeDtypeStruct(adj.shape, adj.dtype),
        in_specs=[vmem] * 5,
        out_specs=vmem,
        cost_estimate=pl.CostEstimate(flops=40 * n, bytes_accessed=12 * n, transcendentals=0),
    )(adj, inputs, alpha, solid, floor)


def whole_grid_body(
    saved_velocity_trajectory,
    saved_warmth_trajectory,
    control_porosity,
    control_volume_flag,
    entrance_face_flag,
):
    lanes = saved_warmth_trajectory.shape[1]
    steps = saved_warmth_trajectory.shape[0]
    me = lax.axis_index("space")

    stacked = jnp.concatenate(
        [saved_velocity_trajectory, saved_warmth_trajectory[:, None]], axis=1
    )
    inputs_all = [None] * steps
    chunk = 2 if steps % 2 == 0 else 1
    near_all = swap_over(stacked, 1)
    for top in range(steps, 0, -chunk):
        own = stacked[top - chunk:top]
        far = swap_over(own, 2)
        relay = swap_over(far, 1)
        piece = in_space_order(me, 2, own, near_all[top - chunk:top], far, relay)
        for j in range(chunk):
            inputs_all[top - chunk + j] = piece[j]

    own_gamma = jnp.where(control_volume_flag == 1, control_porosity, jnp.float32(0.0))
    gamma = gathered_cells(own_gamma, me, 0)
    solid = 1.0 - gamma
    alpha = 3.0 * 0.1 * solid / (0.1 + gamma)
    own_flag = control_volume_flag.astype(jnp.float32)
    own_sensitivity = -3.0 * 0.1 * 1.1 / ((0.1 + own_gamma) * (0.1 + own_gamma))

    floor = entrance_face_flag.astype(jnp.float32)

    def one_step(adj, s):
        return kernel_step(adj, inputs_all[s], alpha, solid, floor)

    def own_cells(x, axis):
        return lax.dynamic_slice_in_dim(x, me * lanes, lanes, axis)

    def sensitivity(adj, s):
        a_loc = own_cells(adj[:3], 1)
        b_loc = own_cells(adj[3], 0)
        speed = saved_velocity_trajectory[s].astype(jnp.float32)
        thermal = saved_warmth_trajectory[s].astype(jnp.float32)
        dot = jnp.sum(a_loc * speed, axis=0)
        return 0.1 * own_flag * (own_sensitivity * dot + 2.0 * (b_loc - 1.0) * thermal)

    grid_shape = (4,) + gamma.shape
    adj = jnp.zeros(grid_shape, jnp.float32)
    for s in range(steps - 1, -1, -1):
        adj = one_step(adj, s)

    core = me % 2
    half = adj.shape[0] // 2
    mine = lax.dynamic_slice_in_dim(adj, core * half, half, 0)
    arrived = passed_along(mine, "arc", -1)
    space_count = lax.axis_size("space")
    swap = [(i, i ^ 1) for i in range(space_count)]
    other = lax.ppermute(arrived, "space", swap)
    adj = jnp.where(
        core == 0,
        jnp.concatenate([arrived, other], axis=0),
        jnp.concatenate([other, arrived], axis=0),
    )

    partial_sum = jnp.zeros(control_porosity.shape, jnp.float32)
    for s in range(steps - 1, -1, -1):
        partial_sum = partial_sum + sensitivity(adj, s)
        adj = one_step(adj, s)

    arcs = lax.axis_size("arc")
    k = lax.axis_index("arc")
    share = partial_sum.shape[1] // arcs
    pieces = partial_sum.reshape(partial_sum.shape[0], arcs, share, partial_sum.shape[2])
    total = lax.dynamic_index_in_dim(pieces, k, 1, keepdims=False)
    for shift in range(1, arcs):
        piece = lax.dynamic_index_in_dim(pieces, (k + shift) % arcs, 1, keepdims=False)
        total = total + passed_along(piece, "arc", shift)
    entry = own_cells(adj, 1)
    return (total, entry[None])


def solution(mesh):
    chosen = whole_grid_body if mesh.shape["space"] == 4 else halo_body
    return jax.shard_map(
        chosen,
        mesh=mesh,
        in_specs=(
            P(("job", "arc"), None, "space", None, None),
            P(("job", "arc"), "space", None, None),
            P(("job", "space"), None, None),
            P(("job", "space"), None, None),
            P("job", None),
        ),
        out_specs=(P(("job", "space"), "arc", None), P(("job", "arc"), None, "space", None, None)),
        check_vma=False,
    )
```

```python
import jax
import jax.numpy as jnp
from jax import lax
from jax.sharding import PartitionSpec as P


def padded(cells, sides, width):
    for axis, dim in sides:
        count = lax.axis_size(axis)
        ends = count - 1
        head = lax.slice_in_dim(cells, 0, width, axis=dim)
        tail = lax.slice_in_dim(cells, cells.shape[dim] - width, cells.shape[dim], axis=dim)
        cells = jnp.concatenate(
            [
                lax.ppermute(tail, axis, [(i, (i + 1) % count) for i in range(ends)]),
                cells,
                lax.ppermute(head, axis, [((i + 1) % count, i) for i in range(ends)]),
            ],
            axis=dim,
        )
    return cells


def passed_along(value, axis, steps):
    count = lax.axis_size(axis)
    pairs = [(source, (source + steps) % count) for source in range(count)]
    return lax.ppermute(value, axis, pairs)


def laplace(ext):
    mid = ext[..., 1:-1, 1:-1, 1:-1]
    total = ext[..., 2:, 1:-1, 1:-1] + ext[..., :-2, 1:-1, 1:-1]
    total = total + ext[..., 1:-1, 2:, 1:-1] + ext[..., 1:-1, :-2, 1:-1]
    total = total + ext[..., 1:-1, 1:-1, 2:] + ext[..., 1:-1, 1:-1, :-2]
    return total - 6.0 * mid


def slopes(ext):
    return (
        0.5 * (ext[..., 2:, 1:-1, 1:-1] - ext[..., :-2, 1:-1, 1:-1]),
        0.5 * (ext[..., 1:-1, 2:, 1:-1] - ext[..., 1:-1, :-2, 1:-1]),
        0.5 * (ext[..., 1:-1, 1:-1, 2:] - ext[..., 1:-1, 1:-1, :-2]),
    )


def pad_sides(field, operating_variant):
    widths = [(0, 0)] * (field.ndim - 2) + [(1, 1), (1, 1)]
    return jnp.pad(field, widths, mode=operating_variant)


def adjoint_update(
    adj,
    ext_a,
    ext_b,
    padded_thermal_field,
    speed,
    alpha,
    porosity_sensitivity,
    solid,
    quadrature_factor,
):
    a_now = adj[:3]
    current_adjoint_vector = adj[3]
    grad_b = slopes(ext_b)
    grad_a = slopes(ext_a)
    grad_t = slopes(padded_thermal_field)
    carry_b = speed[0] * grad_b[0] + speed[1] * grad_b[1] + speed[2] * grad_b[2]
    carry_a = speed[0:1] * grad_a[0] + speed[1:2] * grad_a[1] + speed[2:3] * grad_a[2]
    thermal_current_field = padded_thermal_field[1:-1, 1:-1, 1:-1]
    grad_stack = jnp.stack(grad_t)
    new_a = a_now + 0.1 * (
        1.2 * laplace(ext_a) + carry_a - alpha * a_now - current_adjoint_vector * grad_stack
    )
    new_b = current_adjoint_vector + 0.1 * (
        1.2 * laplace(ext_b) + carry_b - 2.0 * solid * current_adjoint_vector + 2.0 * solid
    )
    common_divisor_lcm_like = jnp.sum(a_now * speed, axis=0)
    summand_contribution = (
        0.1
        * quadrature_factor
        * (
            porosity_sensitivity * common_divisor_lcm_like
            + 2.0 * (current_adjoint_vector - 1.0) * thermal_current_field
        )
    )
    return (jnp.concatenate([new_a, new_b[None]], axis=0), summand_contribution)


def halo_body(
    saved_velocity_trajectory,
    saved_warmth_trajectory,
    control_porosity,
    control_volume_flag,
    entrance_face_flag,
):
    quadrature_factor = control_volume_flag.astype(jnp.float32)
    gamma = jnp.where(control_volume_flag == 1, control_porosity, jnp.float32(0.0))
    solid = 1.0 - gamma
    alpha = 3.0 * 0.1 * solid / (0.1 + gamma)
    porosity_sensitivity = -3.0 * 0.1 * 1.1 / ((0.1 + gamma) * (0.1 + gamma))
    leading_plane = lax.axis_index("space") == 0
    trailing_plane = lax.axis_index("space") == lax.axis_size("space") - 1
    device_instant_total = saved_warmth_trajectory.shape[0]
    cycle_ext = padded(saved_warmth_trajectory, (("space", 1),), 1)

    def closing_thermal_value(thermal_current_field, with_halo_padding):
        floor_limit = jnp.where(leading_plane, thermal_current_field[0], with_halo_padding[0])
        ceiling_bound = jnp.where(trailing_plane, thermal_current_field[-1], with_halo_padding[-1])
        return pad_sides(
            jnp.concatenate(
                [floor_limit[None], thermal_current_field, ceiling_bound[None]], axis=0
            ),
            "edge",
        )

    def one_step(adj, interior_block):
        speed = saved_velocity_trajectory[interior_block].astype(jnp.float32)
        thermal_current_field = saved_warmth_trajectory[interior_block].astype(jnp.float32)
        with_halo_padding = padded(adj, (("space", 1),), 1)
        thermal_halo_values = cycle_ext[interior_block].astype(jnp.float32)
        complete_thermal_field = jnp.concatenate(
            [thermal_halo_values[:1], thermal_current_field, thermal_halo_values[-1:]], axis=0
        )
        padded_thermal_field = closing_thermal_value(thermal_current_field, complete_thermal_field)
        ext_a = pad_sides(with_halo_padding[:3], "constant")
        current_adjoint_vector = adj[3]
        floor_limit = jnp.where(
            leading_plane,
            jnp.where(entrance_face_flag == 1, jnp.float32(0.0), current_adjoint_vector[0]),
            with_halo_padding[3, 0],
        )
        ceiling_bound = jnp.where(
            trailing_plane, current_adjoint_vector[-1], with_halo_padding[3, -1]
        )
        ext_b = pad_sides(
            jnp.concatenate(
                [floor_limit[None], current_adjoint_vector, ceiling_bound[None]], axis=0
            ),
            "edge",
        )
        return adjoint_update(
            adj,
            ext_a,
            ext_b,
            padded_thermal_field,
            speed,
            alpha,
            porosity_sensitivity,
            solid,
            quadrature_factor,
        )

    grid_shape = (4,) + control_porosity.shape
    adj = jnp.zeros(grid_shape, jnp.float32)
    for interior_block in range(device_instant_total - 1, -1, -1):
        adj, unused = one_step(adj, interior_block)
    adj = passed_along(adj, "arc", -1)
    partial_sum = jnp.zeros(control_porosity.shape, jnp.float32)
    for interior_block in range(device_instant_total - 1, -1, -1):
        adj, summand_contribution = one_step(adj, interior_block)
        partial_sum = partial_sum + summand_contribution
    summed = lax.psum(partial_sum, "arc")
    share = summed.shape[1] // lax.axis_size("arc")
    gradient = lax.dynamic_slice_in_dim(summed, lax.axis_index("arc") * share, share, 1)
    return (gradient, adj[None])


def swap_over(value, partner_bit):
    count = lax.axis_size("space")
    return lax.ppermute(value, "space", [(i, i ^ partner_bit) for i in range(count)])


def in_space_order(me, axis, own, near, far, relay):
    pieces = [own, near, far, relay]
    odd = (me & 1) == 1
    pieces = [
        jnp.where(odd, pieces[1], pieces[0]),
        jnp.where(odd, pieces[0], pieces[1]),
        jnp.where(odd, pieces[3], pieces[2]),
        jnp.where(odd, pieces[2], pieces[3]),
    ]
    high = (me & 2) == 2
    pieces = [
        jnp.where(high, pieces[2], pieces[0]),
        jnp.where(high, pieces[3], pieces[1]),
        jnp.where(high, pieces[0], pieces[2]),
        jnp.where(high, pieces[1], pieces[3]),
    ]
    return jnp.concatenate(pieces, axis=axis)


def gathered_cells(local, me, axis):
    near = swap_over(local, 1)
    far = swap_over(local, 2)
    relay = swap_over(far, 1)
    return in_space_order(me, axis, local, near, far, relay)


def whole_grid_body(
    saved_velocity_trajectory,
    saved_warmth_trajectory,
    control_porosity,
    control_volume_flag,
    entrance_face_flag,
):
    lanes = saved_warmth_trajectory.shape[1]
    steps = saved_warmth_trajectory.shape[0]
    me = lax.axis_index("space")

    stacked = jnp.concatenate(
        [saved_velocity_trajectory, saved_warmth_trajectory[:, None]], axis=1
    )
    inputs_all = [None] * steps
    chunk = 2 if steps % 2 == 0 else 1
    near_all = swap_over(stacked, 1)
    for top in range(steps, 0, -chunk):
        own = stacked[top - chunk:top]
        far = swap_over(own, 2)
        relay = swap_over(far, 1)
        piece = in_space_order(me, 2, own, near_all[top - chunk:top], far, relay)
        for j in range(chunk):
            inputs_all[top - chunk + j] = piece[j]

    own_gamma = jnp.where(control_volume_flag == 1, control_porosity, jnp.float32(0.0))
    gamma = gathered_cells(own_gamma, me, 0)
    solid = 1.0 - gamma
    alpha = 3.0 * 0.1 * solid / (0.1 + gamma)
    own_flag = control_volume_flag.astype(jnp.float32)
    own_sensitivity = -3.0 * 0.1 * 1.1 / ((0.1 + own_gamma) * (0.1 + own_gamma))

    def one_step(adj, s):
        speed = inputs_all[s][:3].astype(jnp.float32)
        thermal = inputs_all[s][3].astype(jnp.float32)
        padded_thermal = jnp.pad(thermal, 1, mode="edge")
        ext_a = jnp.pad(adj[:3], ((0, 0), (1, 1), (1, 1), (1, 1)))
        b = adj[3]
        floor_limit = jnp.where(entrance_face_flag == 1, jnp.float32(0.0), b[0])
        ext_b = pad_sides(jnp.concatenate([floor_limit[None], b, b[-1][None]], axis=0), "edge")
        a_now = adj[:3]
        grad_b = slopes(ext_b)
        grad_a = slopes(ext_a)
        grad_t = slopes(padded_thermal)
        carry_b = speed[0] * grad_b[0] + speed[1] * grad_b[1] + speed[2] * grad_b[2]
        carry_a = speed[0:1] * grad_a[0] + speed[1:2] * grad_a[1] + speed[2:3] * grad_a[2]
        new_a = a_now + 0.1 * (
            1.2 * laplace(ext_a) + carry_a - alpha * a_now - b * jnp.stack(grad_t)
        )
        new_b = b + 0.1 * (1.2 * laplace(ext_b) + carry_b - 2.0 * solid * b + 2.0 * solid)
        return jnp.concatenate([new_a, new_b[None]], axis=0)

    def own_cells(x, axis):
        return lax.dynamic_slice_in_dim(x, me * lanes, lanes, axis)

    def sensitivity(adj, s):
        a_loc = own_cells(adj[:3], 1)
        b_loc = own_cells(adj[3], 0)
        speed = saved_velocity_trajectory[s].astype(jnp.float32)
        thermal = saved_warmth_trajectory[s].astype(jnp.float32)
        dot = jnp.sum(a_loc * speed, axis=0)
        return 0.1 * own_flag * (own_sensitivity * dot + 2.0 * (b_loc - 1.0) * thermal)

    grid_shape = (4,) + gamma.shape
    adj = jnp.zeros(grid_shape, jnp.float32)
    for s in range(steps - 1, -1, -1):
        adj = one_step(adj, s)

    mine = own_cells(adj, 1)
    half = mine.shape[0] // 2
    first = passed_along(mine[:half], "arc", -1)
    anchor = jnp.float32(0.0) * first[0, 0, 0, 0]
    second = passed_along(mine[half:] + anchor, "arc", -1)
    adj = jnp.concatenate(
        [gathered_cells(first, me, 1), gathered_cells(second, me, 1)], axis=0
    )

    partial_sum = jnp.zeros(control_porosity.shape, jnp.float32)
    for s in range(steps - 1, -1, -1):
        partial_sum = partial_sum + sensitivity(adj, s)
        adj = one_step(adj, s)

    arcs = lax.axis_size("arc")
    k = lax.axis_index("arc")
    share = partial_sum.shape[1] // arcs
    pieces = partial_sum.reshape(partial_sum.shape[0], arcs, share, partial_sum.shape[2])
    total = lax.dynamic_index_in_dim(pieces, k, 1, keepdims=False)
    for shift in range(1, arcs):
        piece = lax.dynamic_index_in_dim(pieces, (k + shift) % arcs, 1, keepdims=False)
        total = total + passed_along(piece, "arc", shift)
    entry = own_cells(adj, 1)
    return (total, entry[None])


def solution(mesh):
    chosen = whole_grid_body if mesh.shape["space"] == 4 else halo_body
    return jax.shard_map(
        chosen,
        mesh=mesh,
        in_specs=(
            P(("job", "arc"), None, "space", None, None),
            P(("job", "arc"), "space", None, None),
            P(("job", "space"), None, None),
            P(("job", "space"), None, None),
            P("job", None),
        ),
        out_specs=(P(("job", "space"), "arc", None), P(("job", "arc"), None, "space", None, None)),
        check_vma=False,
    )
```

```python
import jax
import jax.numpy as jnp
from jax import lax
from jax.experimental import pallas as pl
from jax.experimental.pallas import tpu as pltpu
from jax.sharding import PartitionSpec as P


def padded(cells, sides, width):
    for axis, dim in sides:
        count = lax.axis_size(axis)
        ends = count - 1
        head = lax.slice_in_dim(cells, 0, width, axis=dim)
        tail = lax.slice_in_dim(cells, cells.shape[dim] - width, cells.shape[dim], axis=dim)
        cells = jnp.concatenate(
            [
                lax.ppermute(tail, axis, [(i, (i + 1) % count) for i in range(ends)]),
                cells,
                lax.ppermute(head, axis, [((i + 1) % count, i) for i in range(ends)]),
            ],
            axis=dim,
        )
    return cells


def passed_along(value, axis, steps):
    count = lax.axis_size(axis)
    pairs = [(source, (source + steps) % count) for source in range(count)]
    return lax.ppermute(value, axis, pairs)


def laplace(ext):
    mid = ext[..., 1:-1, 1:-1, 1:-1]
    total = ext[..., 2:, 1:-1, 1:-1] + ext[..., :-2, 1:-1, 1:-1]
    total = total + ext[..., 1:-1, 2:, 1:-1] + ext[..., 1:-1, :-2, 1:-1]
    total = total + ext[..., 1:-1, 1:-1, 2:] + ext[..., 1:-1, 1:-1, :-2]
    return total - 6.0 * mid


def slopes(ext):
    return (
        0.5 * (ext[..., 2:, 1:-1, 1:-1] - ext[..., :-2, 1:-1, 1:-1]),
        0.5 * (ext[..., 1:-1, 2:, 1:-1] - ext[..., 1:-1, :-2, 1:-1]),
        0.5 * (ext[..., 1:-1, 1:-1, 2:] - ext[..., 1:-1, 1:-1, :-2]),
    )


def pad_sides(field, operating_variant):
    widths = [(0, 0)] * (field.ndim - 2) + [(1, 1), (1, 1)]
    return jnp.pad(field, widths, mode=operating_variant)


def adjoint_update(
    adj,
    ext_a,
    ext_b,
    padded_thermal_field,
    speed,
    alpha,
    porosity_sensitivity,
    solid,
    quadrature_factor,
):
    a_now = adj[:3]
    current_adjoint_vector = adj[3]
    grad_b = slopes(ext_b)
    grad_a = slopes(ext_a)
    grad_t = slopes(padded_thermal_field)
    carry_b = speed[0] * grad_b[0] + speed[1] * grad_b[1] + speed[2] * grad_b[2]
    carry_a = speed[0:1] * grad_a[0] + speed[1:2] * grad_a[1] + speed[2:3] * grad_a[2]
    thermal_current_field = padded_thermal_field[1:-1, 1:-1, 1:-1]
    grad_stack = jnp.stack(grad_t)
    new_a = a_now + 0.1 * (
        1.2 * laplace(ext_a) + carry_a - alpha * a_now - current_adjoint_vector * grad_stack
    )
    new_b = current_adjoint_vector + 0.1 * (
        1.2 * laplace(ext_b) + carry_b - 2.0 * solid * current_adjoint_vector + 2.0 * solid
    )
    common_divisor_lcm_like = jnp.sum(a_now * speed, axis=0)
    summand_contribution = (
        0.1
        * quadrature_factor
        * (
            porosity_sensitivity * common_divisor_lcm_like
            + 2.0 * (current_adjoint_vector - 1.0) * thermal_current_field
        )
    )
    return (jnp.concatenate([new_a, new_b[None]], axis=0), summand_contribution)


def halo_body(
    saved_velocity_trajectory,
    saved_warmth_trajectory,
    control_porosity,
    control_volume_flag,
    entrance_face_flag,
):
    quadrature_factor = control_volume_flag.astype(jnp.float32)
    gamma = jnp.where(control_volume_flag == 1, control_porosity, jnp.float32(0.0))
    solid = 1.0 - gamma
    alpha = 3.0 * 0.1 * solid / (0.1 + gamma)
    porosity_sensitivity = -3.0 * 0.1 * 1.1 / ((0.1 + gamma) * (0.1 + gamma))
    leading_plane = lax.axis_index("space") == 0
    trailing_plane = lax.axis_index("space") == lax.axis_size("space") - 1
    device_instant_total = saved_warmth_trajectory.shape[0]
    cycle_ext = padded(saved_warmth_trajectory, (("space", 1),), 1)

    def closing_thermal_value(thermal_current_field, with_halo_padding):
        floor_limit = jnp.where(leading_plane, thermal_current_field[0], with_halo_padding[0])
        ceiling_bound = jnp.where(trailing_plane, thermal_current_field[-1], with_halo_padding[-1])
        return pad_sides(
            jnp.concatenate(
                [floor_limit[None], thermal_current_field, ceiling_bound[None]], axis=0
            ),
            "edge",
        )

    def one_step(adj, interior_block):
        speed = saved_velocity_trajectory[interior_block].astype(jnp.float32)
        thermal_current_field = saved_warmth_trajectory[interior_block].astype(jnp.float32)
        with_halo_padding = padded(adj, (("space", 1),), 1)
        thermal_halo_values = cycle_ext[interior_block].astype(jnp.float32)
        complete_thermal_field = jnp.concatenate(
            [thermal_halo_values[:1], thermal_current_field, thermal_halo_values[-1:]], axis=0
        )
        padded_thermal_field = closing_thermal_value(thermal_current_field, complete_thermal_field)
        ext_a = pad_sides(with_halo_padding[:3], "constant")
        current_adjoint_vector = adj[3]
        floor_limit = jnp.where(
            leading_plane,
            jnp.where(entrance_face_flag == 1, jnp.float32(0.0), current_adjoint_vector[0]),
            with_halo_padding[3, 0],
        )
        ceiling_bound = jnp.where(
            trailing_plane, current_adjoint_vector[-1], with_halo_padding[3, -1]
        )
        ext_b = pad_sides(
            jnp.concatenate(
                [floor_limit[None], current_adjoint_vector, ceiling_bound[None]], axis=0
            ),
            "edge",
        )
        return adjoint_update(
            adj,
            ext_a,
            ext_b,
            padded_thermal_field,
            speed,
            alpha,
            porosity_sensitivity,
            solid,
            quadrature_factor,
        )

    grid_shape = (4,) + control_porosity.shape
    adj = jnp.zeros(grid_shape, jnp.float32)
    for interior_block in range(device_instant_total - 1, -1, -1):
        adj, unused = one_step(adj, interior_block)
    adj = passed_along(adj, "arc", -1)
    partial_sum = jnp.zeros(control_porosity.shape, jnp.float32)
    for interior_block in range(device_instant_total - 1, -1, -1):
        adj, summand_contribution = one_step(adj, interior_block)
        partial_sum = partial_sum + summand_contribution
    summed = lax.psum(partial_sum, "arc")
    share = summed.shape[1] // lax.axis_size("arc")
    gradient = lax.dynamic_slice_in_dim(summed, lax.axis_index("arc") * share, share, 1)
    return (gradient, adj[None])


def swap_over(value, partner_bit):
    count = lax.axis_size("space")
    return lax.ppermute(value, "space", [(i, i ^ partner_bit) for i in range(count)])


def in_space_order(me, axis, own, near, far, relay):
    pieces = [own, near, far, relay]
    odd = (me & 1) == 1
    pieces = [
        jnp.where(odd, pieces[1], pieces[0]),
        jnp.where(odd, pieces[0], pieces[1]),
        jnp.where(odd, pieces[3], pieces[2]),
        jnp.where(odd, pieces[2], pieces[3]),
    ]
    high = (me & 2) == 2
    pieces = [
        jnp.where(high, pieces[2], pieces[0]),
        jnp.where(high, pieces[3], pieces[1]),
        jnp.where(high, pieces[0], pieces[2]),
        jnp.where(high, pieces[1], pieces[3]),
    ]
    return jnp.concatenate(pieces, axis=axis)


def gathered_cells(local, me, axis):
    near = swap_over(local, 1)
    far = swap_over(local, 2)
    relay = swap_over(far, 1)
    return in_space_order(me, axis, local, near, far, relay)


def _lane_pair(f, edge):
    n = f.shape[1]
    lane = lax.broadcasted_iota(jnp.int32, f.shape, 1)
    up = jnp.where(lane == n - 1, f if edge else 0.0, pltpu.roll(f, n - 1, 1))
    down = jnp.where(lane == 0, f if edge else 0.0, pltpu.roll(f, 1, 1))
    return up, down


def _row_pair(f, before, after, first, last, edge):
    n = f.shape[0]
    row = lax.broadcasted_iota(jnp.int32, f.shape, 0)
    up = jnp.where(row == n - 1, pltpu.roll(after, n - 1, 0), pltpu.roll(f, n - 1, 0))
    down = jnp.where(row == 0, pltpu.roll(before, 1, 0), pltpu.roll(f, 1, 0))
    up = jnp.where(last & (row == n - 1), f if edge else 0.0, up)
    down = jnp.where(first & (row == 0), f if edge else 0.0, down)
    return up, down


STRIP = 16


def _strip_kernel(adj_ref, inp_ref, alpha_ref, solid_ref, ent_ref, out_ref):
    cells = adj_ref.shape[1]
    strips = adj_ref.shape[2] // STRIP

    def body(n, carry):
        i = n // strips
        k = n % strips
        hi = jnp.minimum(i + 1, cells - 1)
        lo = jnp.maximum(i - 1, 0)
        rows = pl.ds(pl.multiple_of(k * STRIP, STRIP), STRIP)
        before = pl.ds(pl.multiple_of(jnp.maximum(k - 1, 0) * STRIP, STRIP), STRIP)
        after = pl.ds(pl.multiple_of(jnp.minimum(k + 1, strips - 1) * STRIP, STRIP), STRIP)
        first = k == 0
        last = k == strips - 1
        top_plane = i == cells - 1
        bottom_plane = i == 0

        def field(ref, c, cast):
            g = lambda p, r: ref[c, p, r, :].astype(jnp.float32) if cast else ref[c, p, r, :]
            return g(i, rows), g(hi, rows), g(lo, rows), g(i, before), g(i, after)

        u = [inp_ref[d, i, rows, :].astype(jnp.float32) for d in range(3)]
        t, t_hi, t_lo, t_b, t_a = field(inp_ref, 3, True)
        t_r = _row_pair(t, t_b, t_a, first, last, True)
        t_l = _lane_pair(t, True)
        grad_t = (0.5 * (t_hi - t_lo), 0.5 * (t_r[0] - t_r[1]), 0.5 * (t_l[0] - t_l[1]))
        b, b_hi, b_lo, b_b, b_a = field(adj_ref, 3, False)
        b_lo = jnp.where(bottom_plane & (ent_ref[rows, :] == 1.0), 0.0, b_lo)
        alpha = alpha_ref[i, rows, :]
        solid = solid_ref[i, rows, :]
        for c in range(3):
            a, a_hi, a_lo, a_b, a_a = field(adj_ref, c, False)
            a_hi = jnp.where(top_plane, 0.0, a_hi)
            a_lo = jnp.where(bottom_plane, 0.0, a_lo)
            a_r = _row_pair(a, a_b, a_a, first, last, False)
            a_l = _lane_pair(a, False)
            lap = (a_hi + a_lo) + a_r[0] + a_r[1] + a_l[0] + a_l[1] - 6.0 * a
            carry_a = (
                u[0] * (0.5 * (a_hi - a_lo))
                + u[1] * (0.5 * (a_r[0] - a_r[1]))
                + u[2] * (0.5 * (a_l[0] - a_l[1]))
            )
            out_ref[c, i, rows, :] = a + 0.1 * (1.2 * lap + carry_a - alpha * a - b * grad_t[c])
        b_r = _row_pair(b, b_b, b_a, first, last, True)
        b_l = _lane_pair(b, True)
        lap_b = (b_hi + b_lo) + b_r[0] + b_r[1] + b_l[0] + b_l[1] - 6.0 * b
        carry_b = (
            u[0] * (0.5 * (b_hi - b_lo))
            + u[1] * (0.5 * (b_r[0] - b_r[1]))
            + u[2] * (0.5 * (b_l[0] - b_l[1]))
        )
        out_ref[3, i, rows, :] = b + 0.1 * (1.2 * lap_b + carry_b - 2.0 * solid * b + 2.0 * solid)
        return carry

    lax.fori_loop(0, cells * strips, body, 0)


def kernel_step(adj, inputs, alpha, solid, floor):
    vmem = pl.BlockSpec(memory_space=pltpu.VMEM)
    n = adj.size
    return pl.pallas_call(
        _strip_kernel,
        out_shape=jax.ShapeDtypeStruct(adj.shape, adj.dtype),
        in_specs=[vmem] * 5,
        out_specs=vmem,
        cost_estimate=pl.CostEstimate(flops=40 * n, bytes_accessed=12 * n, transcendentals=0),
    )(adj, inputs, alpha, solid, floor)


def whole_grid_body(
    saved_velocity_trajectory,
    saved_warmth_trajectory,
    control_porosity,
    control_volume_flag,
    entrance_face_flag,
):
    lanes = saved_warmth_trajectory.shape[1]
    steps = saved_warmth_trajectory.shape[0]
    me = lax.axis_index("space")

    stacked = jnp.concatenate(
        [saved_velocity_trajectory, saved_warmth_trajectory[:, None]], axis=1
    )
    inputs_all = [None] * steps
    chunk = 2 if steps % 2 == 0 else 1
    near_all = swap_over(stacked, 1)
    for top in range(steps, 0, -chunk):
        own = stacked[top - chunk:top]
        far = swap_over(own, 2)
        relay = swap_over(far, 1)
        piece = in_space_order(me, 2, own, near_all[top - chunk:top], far, relay)
        for j in range(chunk):
            inputs_all[top - chunk + j] = piece[j]

    own_gamma = jnp.where(control_volume_flag == 1, control_porosity, jnp.float32(0.0))
    gamma = gathered_cells(own_gamma, me, 0)
    solid = 1.0 - gamma
    alpha = 3.0 * 0.1 * solid / (0.1 + gamma)
    own_flag = control_volume_flag.astype(jnp.float32)
    own_sensitivity = -3.0 * 0.1 * 1.1 / ((0.1 + own_gamma) * (0.1 + own_gamma))

    floor = entrance_face_flag.astype(jnp.float32)

    def one_step(adj, s):
        return kernel_step(adj, inputs_all[s], alpha, solid, floor)

    def own_cells(x, axis):
        return lax.dynamic_slice_in_dim(x, me * lanes, lanes, axis)

    def sensitivity(adj, s):
        a_loc = own_cells(adj[:3], 1)
        b_loc = own_cells(adj[3], 0)
        speed = saved_velocity_trajectory[s].astype(jnp.float32)
        thermal = saved_warmth_trajectory[s].astype(jnp.float32)
        dot = jnp.sum(a_loc * speed, axis=0)
        return 0.1 * own_flag * (own_sensitivity * dot + 2.0 * (b_loc - 1.0) * thermal)

    grid_shape = (4,) + gamma.shape
    adj = jnp.zeros(grid_shape, jnp.float32)
    for s in range(steps - 1, -1, -1):
        adj = one_step(adj, s)

    core = me % 2
    half = adj.shape[0] // 2
    mine = lax.dynamic_slice_in_dim(adj, core * half, half, 0)
    arrived = passed_along(mine, "arc", -1)
    space_count = lax.axis_size("space")
    swap = [(i, i ^ 1) for i in range(space_count)]
    other = lax.ppermute(arrived, "space", swap)
    adj = jnp.where(
        core == 0,
        jnp.concatenate([arrived, other], axis=0),
        jnp.concatenate([other, arrived], axis=0),
    )

    partial_sum = jnp.zeros(control_porosity.shape, jnp.float32)
    for s in range(steps - 1, -1, -1):
        partial_sum = partial_sum + sensitivity(adj, s)
        adj = one_step(adj, s)

    arcs = lax.axis_size("arc")
    k = lax.axis_index("arc")
    share = partial_sum.shape[1] // arcs
    pieces = partial_sum.reshape(partial_sum.shape[0], arcs, share, partial_sum.shape[2])
    total = lax.dynamic_index_in_dim(pieces, k, 1, keepdims=False)
    for shift in range(1, arcs):
        piece = lax.dynamic_index_in_dim(pieces, (k + shift) % arcs, 1, keepdims=False)
        total = total + passed_along(piece, "arc", shift)
    entry = own_cells(adj, 1)
    return (total, entry[None])


def solution(mesh):
    chosen = whole_grid_body if mesh.shape["space"] == 4 else halo_body
    return jax.shard_map(
        chosen,
        mesh=mesh,
        in_specs=(
            P(("job", "arc"), None, "space", None, None),
            P(("job", "arc"), "space", None, None),
            P(("job", "space"), None, None),
            P(("job", "space"), None, None),
            P("job", None),
        ),
        out_specs=(P(("job", "space"), "arc", None), P(("job", "arc"), None, "space", None, None)),
        check_vma=False,
    )
```

```python
import jax
import jax.numpy as jnp
from jax import lax
from jax.sharding import PartitionSpec as P


def padded(cells, sides, width):
    for axis, dim in sides:
        count = lax.axis_size(axis)
        ends = count - 1
        head = lax.slice_in_dim(cells, 0, width, axis=dim)
        tail = lax.slice_in_dim(cells, cells.shape[dim] - width, cells.shape[dim], axis=dim)
        cells = jnp.concatenate(
            [
                lax.ppermute(tail, axis, [(i, (i + 1) % count) for i in range(ends)]),
                cells,
                lax.ppermute(head, axis, [((i + 1) % count, i) for i in range(ends)]),
            ],
            axis=dim,
        )
    return cells


def passed_along(value, axis, steps):
    count = lax.axis_size(axis)
    pairs = [(source, (source + steps) % count) for source in range(count)]
    return lax.ppermute(value, axis, pairs)


def laplace(ext):
    mid = ext[..., 1:-1, 1:-1, 1:-1]
    total = ext[..., 2:, 1:-1, 1:-1] + ext[..., :-2, 1:-1, 1:-1]
    total = total + ext[..., 1:-1, 2:, 1:-1] + ext[..., 1:-1, :-2, 1:-1]
    total = total + ext[..., 1:-1, 1:-1, 2:] + ext[..., 1:-1, 1:-1, :-2]
    return total - 6.0 * mid


def slopes(ext):
    return (
        0.5 * (ext[..., 2:, 1:-1, 1:-1] - ext[..., :-2, 1:-1, 1:-1]),
        0.5 * (ext[..., 1:-1, 2:, 1:-1] - ext[..., 1:-1, :-2, 1:-1]),
        0.5 * (ext[..., 1:-1, 1:-1, 2:] - ext[..., 1:-1, 1:-1, :-2]),
    )


def pad_sides(field, operating_variant):
    widths = [(0, 0)] * (field.ndim - 2) + [(1, 1), (1, 1)]
    return jnp.pad(field, widths, mode=operating_variant)


def adjoint_update(
    adj,
    ext_a,
    ext_b,
    padded_thermal_field,
    speed,
    alpha,
    porosity_sensitivity,
    solid,
    quadrature_factor,
):
    a_now = adj[:3]
    current_adjoint_vector = adj[3]
    grad_b = slopes(ext_b)
    grad_a = slopes(ext_a)
    grad_t = slopes(padded_thermal_field)
    carry_b = speed[0] * grad_b[0] + speed[1] * grad_b[1] + speed[2] * grad_b[2]
    carry_a = speed[0:1] * grad_a[0] + speed[1:2] * grad_a[1] + speed[2:3] * grad_a[2]
    thermal_current_field = padded_thermal_field[1:-1, 1:-1, 1:-1]
    grad_stack = jnp.stack(grad_t)
    new_a = a_now + 0.1 * (
        1.2 * laplace(ext_a) + carry_a - alpha * a_now - current_adjoint_vector * grad_stack
    )
    new_b = current_adjoint_vector + 0.1 * (
        1.2 * laplace(ext_b) + carry_b - 2.0 * solid * current_adjoint_vector + 2.0 * solid
    )
    common_divisor_lcm_like = jnp.sum(a_now * speed, axis=0)
    summand_contribution = (
        0.1
        * quadrature_factor
        * (
            porosity_sensitivity * common_divisor_lcm_like
            + 2.0 * (current_adjoint_vector - 1.0) * thermal_current_field
        )
    )
    return (jnp.concatenate([new_a, new_b[None]], axis=0), summand_contribution)


def halo_body(
    saved_velocity_trajectory,
    saved_warmth_trajectory,
    control_porosity,
    control_volume_flag,
    entrance_face_flag,
):
    quadrature_factor = control_volume_flag.astype(jnp.float32)
    gamma = jnp.where(control_volume_flag == 1, control_porosity, jnp.float32(0.0))
    solid = 1.0 - gamma
    alpha = 3.0 * 0.1 * solid / (0.1 + gamma)
    porosity_sensitivity = -3.0 * 0.1 * 1.1 / ((0.1 + gamma) * (0.1 + gamma))
    leading_plane = lax.axis_index("space") == 0
    trailing_plane = lax.axis_index("space") == lax.axis_size("space") - 1
    device_instant_total = saved_warmth_trajectory.shape[0]
    cycle_ext = padded(saved_warmth_trajectory, (("space", 1),), 1)

    def closing_thermal_value(thermal_current_field, with_halo_padding):
        floor_limit = jnp.where(leading_plane, thermal_current_field[0], with_halo_padding[0])
        ceiling_bound = jnp.where(trailing_plane, thermal_current_field[-1], with_halo_padding[-1])
        return pad_sides(
            jnp.concatenate(
                [floor_limit[None], thermal_current_field, ceiling_bound[None]], axis=0
            ),
            "edge",
        )

    def one_step(adj, interior_block):
        speed = saved_velocity_trajectory[interior_block].astype(jnp.float32)
        thermal_current_field = saved_warmth_trajectory[interior_block].astype(jnp.float32)
        with_halo_padding = padded(adj, (("space", 1),), 1)
        thermal_halo_values = cycle_ext[interior_block].astype(jnp.float32)
        complete_thermal_field = jnp.concatenate(
            [thermal_halo_values[:1], thermal_current_field, thermal_halo_values[-1:]], axis=0
        )
        padded_thermal_field = closing_thermal_value(thermal_current_field, complete_thermal_field)
        ext_a = pad_sides(with_halo_padding[:3], "constant")
        current_adjoint_vector = adj[3]
        floor_limit = jnp.where(
            leading_plane,
            jnp.where(entrance_face_flag == 1, jnp.float32(0.0), current_adjoint_vector[0]),
            with_halo_padding[3, 0],
        )
        ceiling_bound = jnp.where(
            trailing_plane, current_adjoint_vector[-1], with_halo_padding[3, -1]
        )
        ext_b = pad_sides(
            jnp.concatenate(
                [floor_limit[None], current_adjoint_vector, ceiling_bound[None]], axis=0
            ),
            "edge",
        )
        return adjoint_update(
            adj,
            ext_a,
            ext_b,
            padded_thermal_field,
            speed,
            alpha,
            porosity_sensitivity,
            solid,
            quadrature_factor,
        )

    grid_shape = (4,) + control_porosity.shape
    adj = jnp.zeros(grid_shape, jnp.float32)
    for interior_block in range(device_instant_total - 1, -1, -1):
        adj, unused = one_step(adj, interior_block)
    adj = passed_along(adj, "arc", -1)
    partial_sum = jnp.zeros(control_porosity.shape, jnp.float32)
    for interior_block in range(device_instant_total - 1, -1, -1):
        adj, summand_contribution = one_step(adj, interior_block)
        partial_sum = partial_sum + summand_contribution
    summed = lax.psum(partial_sum, "arc")
    share = summed.shape[1] // lax.axis_size("arc")
    gradient = lax.dynamic_slice_in_dim(summed, lax.axis_index("arc") * share, share, 1)
    return (gradient, adj[None])


def swap_over(value, partner_bit):
    count = lax.axis_size("space")
    return lax.ppermute(value, "space", [(i, i ^ partner_bit) for i in range(count)])


def in_space_order(me, axis, own, near, far, relay):
    width = own.shape[axis]
    shape = list(own.shape)
    shape[axis] = 4 * width
    whole = jnp.zeros(shape, own.dtype)
    for q, piece in enumerate((own, near, far, relay)):
        whole = lax.dynamic_update_slice_in_dim(whole, piece, (me ^ q) * width, axis)
    return whole


def gathered_cells(local, me, axis):
    near = swap_over(local, 1)
    far = swap_over(local, 2)
    relay = swap_over(far, 1)
    return in_space_order(me, axis, local, near, far, relay)


def whole_grid_body(
    saved_velocity_trajectory,
    saved_warmth_trajectory,
    control_porosity,
    control_volume_flag,
    entrance_face_flag,
):
    lanes = saved_warmth_trajectory.shape[1]
    steps = saved_warmth_trajectory.shape[0]
    me = lax.axis_index("space")

    inputs_all = [None] * steps
    chunk = 2 if steps % 2 == 0 else 1
    tops = list(range(steps, 0, -chunk))
    stacked = [
        jnp.concatenate(
            [
                saved_velocity_trajectory[top - chunk:top],
                saved_warmth_trajectory[top - chunk:top, None],
            ],
            axis=1,
        )
        for top in tops
    ]
    near_all = swap_over(jnp.concatenate(stacked, axis=0), 1)
    for c, top in enumerate(tops):
        own = stacked[c]
        near = near_all[c * chunk:(c + 1) * chunk]
        far = swap_over(own, 2)
        relay = swap_over(far, 1)
        piece = in_space_order(me, 2, own, near, far, relay)
        for j in range(chunk):
            inputs_all[top - chunk + j] = piece[j]

    own_gamma = jnp.where(control_volume_flag == 1, control_porosity, jnp.float32(0.0))
    gamma = gathered_cells(own_gamma, me, 0)
    solid = 1.0 - gamma
    alpha = 3.0 * 0.1 * solid / (0.1 + gamma)
    own_flag = control_volume_flag.astype(jnp.float32)
    own_sensitivity = -3.0 * 0.1 * 1.1 / ((0.1 + own_gamma) * (0.1 + own_gamma))

    def one_step(adj, s):
        speed = inputs_all[s][:3].astype(jnp.float32)
        thermal = inputs_all[s][3].astype(jnp.float32)
        padded_thermal = jnp.pad(thermal, 1, mode="edge")
        ext_a = jnp.pad(adj[:3], ((0, 0), (1, 1), (1, 1), (1, 1)))
        b = adj[3]
        floor_limit = jnp.where(entrance_face_flag == 1, jnp.float32(0.0), b[0])
        ext_b = pad_sides(jnp.concatenate([floor_limit[None], b, b[-1][None]], axis=0), "edge")
        a_now = adj[:3]
        grad_b = slopes(ext_b)
        grad_a = slopes(ext_a)
        grad_t = slopes(padded_thermal)
        carry_b = speed[0] * grad_b[0] + speed[1] * grad_b[1] + speed[2] * grad_b[2]
        carry_a = speed[0:1] * grad_a[0] + speed[1:2] * grad_a[1] + speed[2:3] * grad_a[2]
        new_a = a_now + 0.1 * (
            1.2 * laplace(ext_a) + carry_a - alpha * a_now - b * jnp.stack(grad_t)
        )
        new_b = b + 0.1 * (1.2 * laplace(ext_b) + carry_b - 2.0 * solid * b + 2.0 * solid)
        return jnp.concatenate([new_a, new_b[None]], axis=0)

    def own_cells(x, axis):
        return lax.dynamic_slice_in_dim(x, me * lanes, lanes, axis)

    def sensitivity(adj, s):
        a_loc = own_cells(adj[:3], 1)
        b_loc = own_cells(adj[3], 0)
        speed = saved_velocity_trajectory[s].astype(jnp.float32)
        thermal = saved_warmth_trajectory[s].astype(jnp.float32)
        dot = jnp.sum(a_loc * speed, axis=0)
        return 0.1 * own_flag * (own_sensitivity * dot + 2.0 * (b_loc - 1.0) * thermal)

    grid_shape = (4,) + gamma.shape
    adj = jnp.zeros(grid_shape, jnp.float32)
    for s in range(steps - 1, -1, -1):
        adj = one_step(adj, s)

    core = me % 2
    half = adj.shape[0] // 2
    mine = lax.dynamic_slice_in_dim(adj, core * half, half, 0)
    arrived = passed_along(mine, "arc", -1)
    space_count = lax.axis_size("space")
    swap = [(i, i ^ 1) for i in range(space_count)]
    other = lax.ppermute(arrived, "space", swap)
    adj = jnp.where(
        core == 0,
        jnp.concatenate([arrived, other], axis=0),
        jnp.concatenate([other, arrived], axis=0),
    )

    partial_sum = jnp.zeros(control_porosity.shape, jnp.float32)
    for s in range(steps - 1, -1, -1):
        partial_sum = partial_sum + sensitivity(adj, s)
        adj = one_step(adj, s)

    arcs = lax.axis_size("arc")
    k = lax.axis_index("arc")
    share = partial_sum.shape[1] // arcs
    pieces = partial_sum.reshape(partial_sum.shape[0], arcs, share, partial_sum.shape[2])
    total = lax.dynamic_index_in_dim(pieces, k, 1, keepdims=False)
    for shift in range(1, arcs):
        piece = lax.dynamic_index_in_dim(pieces, (k + shift) % arcs, 1, keepdims=False)
        total = total + passed_along(piece, "arc", shift)
    entry = own_cells(adj, 1)
    return (total, entry[None])


def solution(mesh):
    chosen = whole_grid_body if mesh.shape["space"] == 4 else halo_body
    return jax.shard_map(
        chosen,
        mesh=mesh,
        in_specs=(
            P(("job", "arc"), None, "space", None, None),
            P(("job", "arc"), "space", None, None),
            P(("job", "space"), None, None),
            P(("job", "space"), None, None),
            P("job", None),
        ),
        out_specs=(P(("job", "space"), "arc", None), P(("job", "arc"), None, "space", None, None)),
        check_vma=False,
    )
```

```python
import jax
import jax.numpy as jnp
from jax import lax
from jax.sharding import PartitionSpec as P


def padded(cells, sides, width):
    for axis, dim in sides:
        count = lax.axis_size(axis)
        ends = count - 1
        head = lax.slice_in_dim(cells, 0, width, axis=dim)
        tail = lax.slice_in_dim(cells, cells.shape[dim] - width, cells.shape[dim], axis=dim)
        cells = jnp.concatenate(
            [
                lax.ppermute(tail, axis, [(i, (i + 1) % count) for i in range(ends)]),
                cells,
                lax.ppermute(head, axis, [((i + 1) % count, i) for i in range(ends)]),
            ],
            axis=dim,
        )
    return cells


def passed_along(value, axis, steps):
    count = lax.axis_size(axis)
    pairs = [(source, (source + steps) % count) for source in range(count)]
    return lax.ppermute(value, axis, pairs)


def laplace(ext):
    mid = ext[..., 1:-1, 1:-1, 1:-1]
    total = ext[..., 2:, 1:-1, 1:-1] + ext[..., :-2, 1:-1, 1:-1]
    total = total + ext[..., 1:-1, 2:, 1:-1] + ext[..., 1:-1, :-2, 1:-1]
    total = total + ext[..., 1:-1, 1:-1, 2:] + ext[..., 1:-1, 1:-1, :-2]
    return total - 6.0 * mid


def slopes(ext):
    return (
        0.5 * (ext[..., 2:, 1:-1, 1:-1] - ext[..., :-2, 1:-1, 1:-1]),
        0.5 * (ext[..., 1:-1, 2:, 1:-1] - ext[..., 1:-1, :-2, 1:-1]),
        0.5 * (ext[..., 1:-1, 1:-1, 2:] - ext[..., 1:-1, 1:-1, :-2]),
    )


def pad_sides(field, operating_variant):
    widths = [(0, 0)] * (field.ndim - 2) + [(1, 1), (1, 1)]
    return jnp.pad(field, widths, mode=operating_variant)


def adjoint_update(
    adj,
    ext_a,
    ext_b,
    padded_thermal_field,
    speed,
    alpha,
    porosity_sensitivity,
    solid,
    quadrature_factor,
):
    a_now = adj[:3]
    current_adjoint_vector = adj[3]
    grad_b = slopes(ext_b)
    grad_a = slopes(ext_a)
    grad_t = slopes(padded_thermal_field)
    carry_b = speed[0] * grad_b[0] + speed[1] * grad_b[1] + speed[2] * grad_b[2]
    carry_a = speed[0:1] * grad_a[0] + speed[1:2] * grad_a[1] + speed[2:3] * grad_a[2]
    thermal_current_field = padded_thermal_field[1:-1, 1:-1, 1:-1]
    grad_stack = jnp.stack(grad_t)
    new_a = a_now + 0.1 * (
        1.2 * laplace(ext_a) + carry_a - alpha * a_now - current_adjoint_vector * grad_stack
    )
    new_b = current_adjoint_vector + 0.1 * (
        1.2 * laplace(ext_b) + carry_b - 2.0 * solid * current_adjoint_vector + 2.0 * solid
    )
    common_divisor_lcm_like = jnp.sum(a_now * speed, axis=0)
    summand_contribution = (
        0.1
        * quadrature_factor
        * (
            porosity_sensitivity * common_divisor_lcm_like
            + 2.0 * (current_adjoint_vector - 1.0) * thermal_current_field
        )
    )
    return (jnp.concatenate([new_a, new_b[None]], axis=0), summand_contribution)


def halo_body(
    saved_velocity_trajectory,
    saved_warmth_trajectory,
    control_porosity,
    control_volume_flag,
    entrance_face_flag,
):
    quadrature_factor = control_volume_flag.astype(jnp.float32)
    gamma = jnp.where(control_volume_flag == 1, control_porosity, jnp.float32(0.0))
    solid = 1.0 - gamma
    alpha = 3.0 * 0.1 * solid / (0.1 + gamma)
    porosity_sensitivity = -3.0 * 0.1 * 1.1 / ((0.1 + gamma) * (0.1 + gamma))
    leading_plane = lax.axis_index("space") == 0
    trailing_plane = lax.axis_index("space") == lax.axis_size("space") - 1
    device_instant_total = saved_warmth_trajectory.shape[0]
    cycle_ext = padded(saved_warmth_trajectory, (("space", 1),), 1)

    def closing_thermal_value(thermal_current_field, with_halo_padding):
        floor_limit = jnp.where(leading_plane, thermal_current_field[0], with_halo_padding[0])
        ceiling_bound = jnp.where(trailing_plane, thermal_current_field[-1], with_halo_padding[-1])
        return pad_sides(
            jnp.concatenate(
                [floor_limit[None], thermal_current_field, ceiling_bound[None]], axis=0
            ),
            "edge",
        )

    def one_step(adj, interior_block):
        speed = saved_velocity_trajectory[interior_block].astype(jnp.float32)
        thermal_current_field = saved_warmth_trajectory[interior_block].astype(jnp.float32)
        with_halo_padding = padded(adj, (("space", 1),), 1)
        thermal_halo_values = cycle_ext[interior_block].astype(jnp.float32)
        complete_thermal_field = jnp.concatenate(
            [thermal_halo_values[:1], thermal_current_field, thermal_halo_values[-1:]], axis=0
        )
        padded_thermal_field = closing_thermal_value(thermal_current_field, complete_thermal_field)
        ext_a = pad_sides(with_halo_padding[:3], "constant")
        current_adjoint_vector = adj[3]
        floor_limit = jnp.where(
            leading_plane,
            jnp.where(entrance_face_flag == 1, jnp.float32(0.0), current_adjoint_vector[0]),
            with_halo_padding[3, 0],
        )
        ceiling_bound = jnp.where(
            trailing_plane, current_adjoint_vector[-1], with_halo_padding[3, -1]
        )
        ext_b = pad_sides(
            jnp.concatenate(
                [floor_limit[None], current_adjoint_vector, ceiling_bound[None]], axis=0
            ),
            "edge",
        )
        return adjoint_update(
            adj,
            ext_a,
            ext_b,
            padded_thermal_field,
            speed,
            alpha,
            porosity_sensitivity,
            solid,
            quadrature_factor,
        )

    grid_shape = (4,) + control_porosity.shape
    adj = jnp.zeros(grid_shape, jnp.float32)
    for interior_block in range(device_instant_total - 1, -1, -1):
        adj, unused = one_step(adj, interior_block)
    adj = passed_along(adj, "arc", -1)
    partial_sum = jnp.zeros(control_porosity.shape, jnp.float32)
    for interior_block in range(device_instant_total - 1, -1, -1):
        adj, summand_contribution = one_step(adj, interior_block)
        partial_sum = partial_sum + summand_contribution
    summed = lax.psum(partial_sum, "arc")
    share = summed.shape[1] // lax.axis_size("arc")
    gradient = lax.dynamic_slice_in_dim(summed, lax.axis_index("arc") * share, share, 1)
    return (gradient, adj[None])


def swap_over(value, partner_bit):
    count = lax.axis_size("space")
    return lax.ppermute(value, "space", [(i, i ^ partner_bit) for i in range(count)])


def in_space_order(me, axis, own, near, far, relay):
    pieces = [own, near, far, relay]
    odd = (me & 1) == 1
    pieces = [
        jnp.where(odd, pieces[1], pieces[0]),
        jnp.where(odd, pieces[0], pieces[1]),
        jnp.where(odd, pieces[3], pieces[2]),
        jnp.where(odd, pieces[2], pieces[3]),
    ]
    high = (me & 2) == 2
    pieces = [
        jnp.where(high, pieces[2], pieces[0]),
        jnp.where(high, pieces[3], pieces[1]),
        jnp.where(high, pieces[0], pieces[2]),
        jnp.where(high, pieces[1], pieces[3]),
    ]
    return jnp.concatenate(pieces, axis=axis)


def gathered_cells(local, me, axis):
    near = swap_over(local, 1)
    far = swap_over(local, 2)
    relay = swap_over(far, 1)
    return in_space_order(me, axis, local, near, far, relay)


def whole_grid_body(
    saved_velocity_trajectory,
    saved_warmth_trajectory,
    control_porosity,
    control_volume_flag,
    entrance_face_flag,
):
    lanes = saved_warmth_trajectory.shape[1]
    steps = saved_warmth_trajectory.shape[0]
    me = lax.axis_index("space")

    stacked = jnp.concatenate(
        [saved_velocity_trajectory, saved_warmth_trajectory[:, None]], axis=1
    )
    inputs_all = [None] * steps
    chunk = 2 if steps % 2 == 0 else 1
    near_all = swap_over(stacked, 1)
    for top in range(steps, 0, -chunk):
        own = stacked[top - chunk:top]
        far = swap_over(own, 2)
        relay = swap_over(far, 1)
        piece = in_space_order(me, 2, own, near_all[top - chunk:top], far, relay)
        for j in range(chunk):
            inputs_all[top - chunk + j] = piece[j]

    own_gamma = jnp.where(control_volume_flag == 1, control_porosity, jnp.float32(0.0))
    gamma = gathered_cells(own_gamma, me, 0)
    solid = 1.0 - gamma
    alpha = 3.0 * 0.1 * solid / (0.1 + gamma)
    own_flag = control_volume_flag.astype(jnp.float32)
    own_sensitivity = -3.0 * 0.1 * 1.1 / ((0.1 + own_gamma) * (0.1 + own_gamma))

    def one_step(adj, s):
        speed = inputs_all[s][:3].astype(jnp.float32)
        thermal = inputs_all[s][3].astype(jnp.float32)
        padded_thermal = jnp.pad(thermal, 1, mode="edge")
        ext_a = jnp.pad(adj[:3], ((0, 0), (1, 1), (1, 1), (1, 1)))
        b = adj[3]
        floor_limit = jnp.where(entrance_face_flag == 1, jnp.float32(0.0), b[0])
        ext_b = pad_sides(jnp.concatenate([floor_limit[None], b, b[-1][None]], axis=0), "edge")
        a_now = adj[:3]
        grad_b = slopes(ext_b)
        grad_a = slopes(ext_a)
        grad_t = slopes(padded_thermal)
        carry_b = speed[0] * grad_b[0] + speed[1] * grad_b[1] + speed[2] * grad_b[2]
        carry_a = speed[0:1] * grad_a[0] + speed[1:2] * grad_a[1] + speed[2:3] * grad_a[2]
        new_a = a_now + 0.1 * (
            1.2 * laplace(ext_a) + carry_a - alpha * a_now - b * jnp.stack(grad_t)
        )
        new_b = b + 0.1 * (1.2 * laplace(ext_b) + carry_b - 2.0 * solid * b + 2.0 * solid)
        return jnp.concatenate([new_a, new_b[None]], axis=0)

    def own_cells(x, axis):
        return lax.dynamic_slice_in_dim(x, me * lanes, lanes, axis)

    def sensitivity(adj, s):
        a_loc = own_cells(adj[:3], 1)
        b_loc = own_cells(adj[3], 0)
        speed = saved_velocity_trajectory[s].astype(jnp.float32)
        thermal = saved_warmth_trajectory[s].astype(jnp.float32)
        dot = jnp.sum(a_loc * speed, axis=0)
        return 0.1 * own_flag * (own_sensitivity * dot + 2.0 * (b_loc - 1.0) * thermal)

    grid_shape = (4,) + gamma.shape
    adj = jnp.zeros(grid_shape, jnp.float32)
    for s in range(steps - 1, -1, -1):
        adj = one_step(adj, s)

    core = me % 2
    half = adj.shape[0] // 2
    mine = lax.dynamic_slice_in_dim(adj, core * half, half, 0)
    arrived = passed_along(mine, "arc", -1)
    space_count = lax.axis_size("space")
    swap = [(i, i ^ 1) for i in range(space_count)]
    other = lax.ppermute(arrived, "space", swap)
    adj = jnp.where(
        core == 0,
        jnp.concatenate([arrived, other], axis=0),
        jnp.concatenate([other, arrived], axis=0),
    )

    partial_sum = jnp.zeros(control_porosity.shape, jnp.float32)
    for s in range(steps - 1, -1, -1):
        partial_sum = partial_sum + sensitivity(adj, s)
        adj = one_step(adj, s)

    arcs = lax.axis_size("arc")
    k = lax.axis_index("arc")
    share = partial_sum.shape[1] // arcs
    pieces = partial_sum.reshape(partial_sum.shape[0], arcs, share, partial_sum.shape[2])
    received = lax.all_to_all(pieces, "arc", 1, 1, tiled=True)
    total = jnp.sum(received, axis=1)
    entry = own_cells(adj, 1)
    return (total, entry[None])


def solution(mesh):
    chosen = whole_grid_body if mesh.shape["space"] == 4 else halo_body
    return jax.shard_map(
        chosen,
        mesh=mesh,
        in_specs=(
            P(("job", "arc"), None, "space", None, None),
            P(("job", "arc"), "space", None, None),
            P(("job", "space"), None, None),
            P(("job", "space"), None, None),
            P("job", None),
        ),
        out_specs=(P(("job", "space"), "arc", None), P(("job", "arc"), None, "space", None, None)),
        check_vma=False,
    )
```

```python
import jax
import jax.numpy as jnp
from jax import lax
from jax.sharding import PartitionSpec as P


def padded(cells, sides, width):
    for axis, dim in sides:
        count = lax.axis_size(axis)
        ends = count - 1
        head = lax.slice_in_dim(cells, 0, width, axis=dim)
        tail = lax.slice_in_dim(cells, cells.shape[dim] - width, cells.shape[dim], axis=dim)
        cells = jnp.concatenate(
            [
                lax.ppermute(tail, axis, [(i, (i + 1) % count) for i in range(ends)]),
                cells,
                lax.ppermute(head, axis, [((i + 1) % count, i) for i in range(ends)]),
            ],
            axis=dim,
        )
    return cells


def passed_along(value, axis, steps):
    count = lax.axis_size(axis)
    pairs = [(source, (source + steps) % count) for source in range(count)]
    return lax.ppermute(value, axis, pairs)


def laplace(ext):
    mid = ext[..., 1:-1, 1:-1, 1:-1]
    total = ext[..., 2:, 1:-1, 1:-1] + ext[..., :-2, 1:-1, 1:-1]
    total = total + ext[..., 1:-1, 2:, 1:-1] + ext[..., 1:-1, :-2, 1:-1]
    total = total + ext[..., 1:-1, 1:-1, 2:] + ext[..., 1:-1, 1:-1, :-2]
    return total - 6.0 * mid


def slopes(ext):
    return (
        0.5 * (ext[..., 2:, 1:-1, 1:-1] - ext[..., :-2, 1:-1, 1:-1]),
        0.5 * (ext[..., 1:-1, 2:, 1:-1] - ext[..., 1:-1, :-2, 1:-1]),
        0.5 * (ext[..., 1:-1, 1:-1, 2:] - ext[..., 1:-1, 1:-1, :-2]),
    )


def pad_sides(field, operating_variant):
    widths = [(0, 0)] * (field.ndim - 2) + [(1, 1), (1, 1)]
    return jnp.pad(field, widths, mode=operating_variant)


def adjoint_update(
    adj,
    ext_a,
    ext_b,
    padded_thermal_field,
    speed,
    alpha,
    porosity_sensitivity,
    solid,
    quadrature_factor,
):
    a_now = adj[:3]
    current_adjoint_vector = adj[3]
    grad_b = slopes(ext_b)
    grad_a = slopes(ext_a)
    grad_t = slopes(padded_thermal_field)
    carry_b = speed[0] * grad_b[0] + speed[1] * grad_b[1] + speed[2] * grad_b[2]
    carry_a = speed[0:1] * grad_a[0] + speed[1:2] * grad_a[1] + speed[2:3] * grad_a[2]
    thermal_current_field = padded_thermal_field[1:-1, 1:-1, 1:-1]
    grad_stack = jnp.stack(grad_t)
    new_a = a_now + 0.1 * (
        1.2 * laplace(ext_a) + carry_a - alpha * a_now - current_adjoint_vector * grad_stack
    )
    new_b = current_adjoint_vector + 0.1 * (
        1.2 * laplace(ext_b) + carry_b - 2.0 * solid * current_adjoint_vector + 2.0 * solid
    )
    common_divisor_lcm_like = jnp.sum(a_now * speed, axis=0)
    summand_contribution = (
        0.1
        * quadrature_factor
        * (
            porosity_sensitivity * common_divisor_lcm_like
            + 2.0 * (current_adjoint_vector - 1.0) * thermal_current_field
        )
    )
    return (jnp.concatenate([new_a, new_b[None]], axis=0), summand_contribution)


def halo_body(
    saved_velocity_trajectory,
    saved_warmth_trajectory,
    control_porosity,
    control_volume_flag,
    entrance_face_flag,
):
    quadrature_factor = control_volume_flag.astype(jnp.float32)
    gamma = jnp.where(control_volume_flag == 1, control_porosity, jnp.float32(0.0))
    solid = 1.0 - gamma
    alpha = 3.0 * 0.1 * solid / (0.1 + gamma)
    porosity_sensitivity = -3.0 * 0.1 * 1.1 / ((0.1 + gamma) * (0.1 + gamma))
    leading_plane = lax.axis_index("space") == 0
    trailing_plane = lax.axis_index("space") == lax.axis_size("space") - 1
    device_instant_total = saved_warmth_trajectory.shape[0]
    cycle_ext = padded(saved_warmth_trajectory, (("space", 1),), 1)

    def closing_thermal_value(thermal_current_field, with_halo_padding):
        floor_limit = jnp.where(leading_plane, thermal_current_field[0], with_halo_padding[0])
        ceiling_bound = jnp.where(trailing_plane, thermal_current_field[-1], with_halo_padding[-1])
        return pad_sides(
            jnp.concatenate(
                [floor_limit[None], thermal_current_field, ceiling_bound[None]], axis=0
            ),
            "edge",
        )

    def one_step(adj, interior_block):
        speed = saved_velocity_trajectory[interior_block].astype(jnp.float32)
        thermal_current_field = saved_warmth_trajectory[interior_block].astype(jnp.float32)
        with_halo_padding = padded(adj, (("space", 1),), 1)
        thermal_halo_values = cycle_ext[interior_block].astype(jnp.float32)
        complete_thermal_field = jnp.concatenate(
            [thermal_halo_values[:1], thermal_current_field, thermal_halo_values[-1:]], axis=0
        )
        padded_thermal_field = closing_thermal_value(thermal_current_field, complete_thermal_field)
        ext_a = pad_sides(with_halo_padding[:3], "constant")
        current_adjoint_vector = adj[3]
        floor_limit = jnp.where(
            leading_plane,
            jnp.where(entrance_face_flag == 1, jnp.float32(0.0), current_adjoint_vector[0]),
            with_halo_padding[3, 0],
        )
        ceiling_bound = jnp.where(
            trailing_plane, current_adjoint_vector[-1], with_halo_padding[3, -1]
        )
        ext_b = pad_sides(
            jnp.concatenate(
                [floor_limit[None], current_adjoint_vector, ceiling_bound[None]], axis=0
            ),
            "edge",
        )
        return adjoint_update(
            adj,
            ext_a,
            ext_b,
            padded_thermal_field,
            speed,
            alpha,
            porosity_sensitivity,
            solid,
            quadrature_factor,
        )

    grid_shape = (4,) + control_porosity.shape
    adj = jnp.zeros(grid_shape, jnp.float32)
    for interior_block in range(device_instant_total - 1, -1, -1):
        adj, unused = one_step(adj, interior_block)
    adj = passed_along(adj, "arc", -1)
    partial_sum = jnp.zeros(control_porosity.shape, jnp.float32)
    for interior_block in range(device_instant_total - 1, -1, -1):
        adj, summand_contribution = one_step(adj, interior_block)
        partial_sum = partial_sum + summand_contribution
    summed = lax.psum(partial_sum, "arc")
    share = summed.shape[1] // lax.axis_size("arc")
    gradient = lax.dynamic_slice_in_dim(summed, lax.axis_index("arc") * share, share, 1)
    return (gradient, adj[None])


def swap_over(value, partner_bit):
    count = lax.axis_size("space")
    return lax.ppermute(value, "space", [(i, i ^ partner_bit) for i in range(count)])


def in_space_order(me, axis, own, near, far, relay):
    pieces = [own, near, far, relay]
    odd = (me & 1) == 1
    pieces = [
        jnp.where(odd, pieces[1], pieces[0]),
        jnp.where(odd, pieces[0], pieces[1]),
        jnp.where(odd, pieces[3], pieces[2]),
        jnp.where(odd, pieces[2], pieces[3]),
    ]
    high = (me & 2) == 2
    pieces = [
        jnp.where(high, pieces[2], pieces[0]),
        jnp.where(high, pieces[3], pieces[1]),
        jnp.where(high, pieces[0], pieces[2]),
        jnp.where(high, pieces[1], pieces[3]),
    ]
    return jnp.concatenate(pieces, axis=axis)


def gathered_cells(local, me, axis):
    near = swap_over(local, 1)
    far = swap_over(local, 2)
    relay = swap_over(far, 1)
    return in_space_order(me, axis, local, near, far, relay)


def whole_grid_body(
    saved_velocity_trajectory,
    saved_warmth_trajectory,
    control_porosity,
    control_volume_flag,
    entrance_face_flag,
):
    lanes = saved_warmth_trajectory.shape[1]
    steps = saved_warmth_trajectory.shape[0]
    me = lax.axis_index("space")

    stacked = jnp.concatenate(
        [saved_velocity_trajectory, saved_warmth_trajectory[:, None]], axis=1
    )
    inputs_all = [None] * steps
    chunk = 2 if steps % 2 == 0 else 1
    near_all = swap_over(stacked, 1)
    for top in range(steps, 0, -chunk):
        own = stacked[top - chunk:top]
        far = swap_over(own, 2)
        relay = swap_over(far, 1)
        piece = in_space_order(me, 2, own, near_all[top - chunk:top], far, relay)
        for j in range(chunk):
            inputs_all[top - chunk + j] = piece[j]

    own_gamma = jnp.where(control_volume_flag == 1, control_porosity, jnp.float32(0.0))
    gamma = gathered_cells(own_gamma, me, 0)
    solid = 1.0 - gamma
    alpha = 3.0 * 0.1 * solid / (0.1 + gamma)
    own_flag = control_volume_flag.astype(jnp.float32)
    own_sensitivity = -3.0 * 0.1 * 1.1 / ((0.1 + own_gamma) * (0.1 + own_gamma))

    def one_step(adj, s):
        speed = inputs_all[s][:3].astype(jnp.float32)
        thermal = inputs_all[s][3].astype(jnp.float32)
        padded_thermal = jnp.pad(thermal, 1, mode="edge")
        ext_a = jnp.pad(adj[:3], ((0, 0), (1, 1), (1, 1), (1, 1)))
        b = adj[3]
        floor_limit = jnp.where(entrance_face_flag == 1, jnp.float32(0.0), b[0])
        ext_b = pad_sides(jnp.concatenate([floor_limit[None], b, b[-1][None]], axis=0), "edge")
        a_now = adj[:3]
        grad_b = slopes(ext_b)
        grad_a = slopes(ext_a)
        grad_t = slopes(padded_thermal)
        carry_b = speed[0] * grad_b[0] + speed[1] * grad_b[1] + speed[2] * grad_b[2]
        carry_a = speed[0:1] * grad_a[0] + speed[1:2] * grad_a[1] + speed[2:3] * grad_a[2]
        new_a = a_now + 0.1 * (
            1.2 * laplace(ext_a) + carry_a - alpha * a_now - b * jnp.stack(grad_t)
        )
        new_b = b + 0.1 * (1.2 * laplace(ext_b) + carry_b - 2.0 * solid * b + 2.0 * solid)
        return jnp.concatenate([new_a, new_b[None]], axis=0)

    def own_cells(x, axis):
        return lax.dynamic_slice_in_dim(x, me * lanes, lanes, axis)

    def sensitivity(adj, s):
        a_loc = own_cells(adj[:3], 1)
        b_loc = own_cells(adj[3], 0)
        speed = saved_velocity_trajectory[s].astype(jnp.float32)
        thermal = saved_warmth_trajectory[s].astype(jnp.float32)
        dot = jnp.sum(a_loc * speed, axis=0)
        return 0.1 * own_flag * (own_sensitivity * dot + 2.0 * (b_loc - 1.0) * thermal)

    grid_shape = (4,) + gamma.shape
    adj = jnp.concatenate(
        [jnp.zeros((3,) + gamma.shape, jnp.float32), (0.1 * (2.0 * solid))[None]], axis=0
    )
    for s in range(steps - 2, -1, -1):
        adj = one_step(adj, s)

    core = me % 2
    half = adj.shape[0] // 2
    mine = lax.dynamic_slice_in_dim(adj, core * half, half, 0)
    arrived = passed_along(mine, "arc", -1)
    space_count = lax.axis_size("space")
    swap = [(i, i ^ 1) for i in range(space_count)]
    other = lax.ppermute(arrived, "space", swap)
    adj = jnp.where(
        core == 0,
        jnp.concatenate([arrived, other], axis=0),
        jnp.concatenate([other, arrived], axis=0),
    )

    partial_sum = jnp.zeros(control_porosity.shape, jnp.float32)
    for s in range(steps - 1, -1, -1):
        partial_sum = partial_sum + sensitivity(adj, s)
        adj = one_step(adj, s)

    arcs = lax.axis_size("arc")
    k = lax.axis_index("arc")
    share = partial_sum.shape[1] // arcs
    pieces = partial_sum.reshape(partial_sum.shape[0], arcs, share, partial_sum.shape[2])
    total = lax.dynamic_index_in_dim(pieces, k, 1, keepdims=False)
    for shift in range(1, arcs):
        piece = lax.dynamic_index_in_dim(pieces, (k + shift) % arcs, 1, keepdims=False)
        total = total + passed_along(piece, "arc", shift)
    entry = own_cells(adj, 1)
    return (total, entry[None])


def solution(mesh):
    chosen = whole_grid_body if mesh.shape["space"] == 4 else halo_body
    return jax.shard_map(
        chosen,
        mesh=mesh,
        in_specs=(
            P(("job", "arc"), None, "space", None, None),
            P(("job", "arc"), "space", None, None),
            P(("job", "space"), None, None),
            P(("job", "space"), None, None),
            P("job", None),
        ),
        out_specs=(P(("job", "space"), "arc", None), P(("job", "arc"), None, "space", None, None)),
        check_vma=False,
    )
```

```python
import jax
import jax.numpy as jnp
from jax import lax
from jax.sharding import PartitionSpec as P


def padded(cells, sides, width):
    for axis, dim in sides:
        count = lax.axis_size(axis)
        ends = count - 1
        head = lax.slice_in_dim(cells, 0, width, axis=dim)
        tail = lax.slice_in_dim(cells, cells.shape[dim] - width, cells.shape[dim], axis=dim)
        cells = jnp.concatenate(
            [
                lax.ppermute(tail, axis, [(i, (i + 1) % count) for i in range(ends)]),
                cells,
                lax.ppermute(head, axis, [((i + 1) % count, i) for i in range(ends)]),
            ],
            axis=dim,
        )
    return cells


def passed_along(value, axis, steps):
    count = lax.axis_size(axis)
    pairs = [(source, (source + steps) % count) for source in range(count)]
    return lax.ppermute(value, axis, pairs)


def laplace(ext):
    mid = ext[..., 1:-1, 1:-1, 1:-1]
    total = ext[..., 2:, 1:-1, 1:-1] + ext[..., :-2, 1:-1, 1:-1]
    total = total + ext[..., 1:-1, 2:, 1:-1] + ext[..., 1:-1, :-2, 1:-1]
    total = total + ext[..., 1:-1, 1:-1, 2:] + ext[..., 1:-1, 1:-1, :-2]
    return total - 6.0 * mid


def slopes(ext):
    return (
        0.5 * (ext[..., 2:, 1:-1, 1:-1] - ext[..., :-2, 1:-1, 1:-1]),
        0.5 * (ext[..., 1:-1, 2:, 1:-1] - ext[..., 1:-1, :-2, 1:-1]),
        0.5 * (ext[..., 1:-1, 1:-1, 2:] - ext[..., 1:-1, 1:-1, :-2]),
    )


def pad_sides(field, operating_variant):
    widths = [(0, 0)] * (field.ndim - 2) + [(1, 1), (1, 1)]
    return jnp.pad(field, widths, mode=operating_variant)


def adjoint_update(
    adj,
    ext_a,
    ext_b,
    padded_thermal_field,
    speed,
    alpha,
    porosity_sensitivity,
    solid,
    quadrature_factor,
):
    a_now = adj[:3]
    current_adjoint_vector = adj[3]
    grad_b = slopes(ext_b)
    grad_a = slopes(ext_a)
    grad_t = slopes(padded_thermal_field)
    carry_b = speed[0] * grad_b[0] + speed[1] * grad_b[1] + speed[2] * grad_b[2]
    carry_a = speed[0:1] * grad_a[0] + speed[1:2] * grad_a[1] + speed[2:3] * grad_a[2]
    thermal_current_field = padded_thermal_field[1:-1, 1:-1, 1:-1]
    grad_stack = jnp.stack(grad_t)
    new_a = a_now + 0.1 * (
        1.2 * laplace(ext_a) + carry_a - alpha * a_now - current_adjoint_vector * grad_stack
    )
    new_b = current_adjoint_vector + 0.1 * (
        1.2 * laplace(ext_b) + carry_b - 2.0 * solid * current_adjoint_vector + 2.0 * solid
    )
    common_divisor_lcm_like = jnp.sum(a_now * speed, axis=0)
    summand_contribution = (
        0.1
        * quadrature_factor
        * (
            porosity_sensitivity * common_divisor_lcm_like
            + 2.0 * (current_adjoint_vector - 1.0) * thermal_current_field
        )
    )
    return (jnp.concatenate([new_a, new_b[None]], axis=0), summand_contribution)


def halo_body(
    saved_velocity_trajectory,
    saved_warmth_trajectory,
    control_porosity,
    control_volume_flag,
    entrance_face_flag,
):
    quadrature_factor = control_volume_flag.astype(jnp.float32)
    gamma = jnp.where(control_volume_flag == 1, control_porosity, jnp.float32(0.0))
    solid = 1.0 - gamma
    alpha = 3.0 * 0.1 * solid / (0.1 + gamma)
    porosity_sensitivity = -3.0 * 0.1 * 1.1 / ((0.1 + gamma) * (0.1 + gamma))
    leading_plane = lax.axis_index("space") == 0
    trailing_plane = lax.axis_index("space") == lax.axis_size("space") - 1
    device_instant_total = saved_warmth_trajectory.shape[0]
    cycle_ext = padded(saved_warmth_trajectory, (("space", 1),), 1)

    def closing_thermal_value(thermal_current_field, with_halo_padding):
        floor_limit = jnp.where(leading_plane, thermal_current_field[0], with_halo_padding[0])
        ceiling_bound = jnp.where(trailing_plane, thermal_current_field[-1], with_halo_padding[-1])
        return pad_sides(
            jnp.concatenate(
                [floor_limit[None], thermal_current_field, ceiling_bound[None]], axis=0
            ),
            "edge",
        )

    def one_step(adj, interior_block):
        speed = saved_velocity_trajectory[interior_block].astype(jnp.float32)
        thermal_current_field = saved_warmth_trajectory[interior_block].astype(jnp.float32)
        with_halo_padding = padded(adj, (("space", 1),), 1)
        thermal_halo_values = cycle_ext[interior_block].astype(jnp.float32)
        complete_thermal_field = jnp.concatenate(
            [thermal_halo_values[:1], thermal_current_field, thermal_halo_values[-1:]], axis=0
        )
        padded_thermal_field = closing_thermal_value(thermal_current_field, complete_thermal_field)
        ext_a = pad_sides(with_halo_padding[:3], "constant")
        current_adjoint_vector = adj[3]
        floor_limit = jnp.where(
            leading_plane,
            jnp.where(entrance_face_flag == 1, jnp.float32(0.0), current_adjoint_vector[0]),
            with_halo_padding[3, 0],
        )
        ceiling_bound = jnp.where(
            trailing_plane, current_adjoint_vector[-1], with_halo_padding[3, -1]
        )
        ext_b = pad_sides(
            jnp.concatenate(
                [floor_limit[None], current_adjoint_vector, ceiling_bound[None]], axis=0
            ),
            "edge",
        )
        return adjoint_update(
            adj,
            ext_a,
            ext_b,
            padded_thermal_field,
            speed,
            alpha,
            porosity_sensitivity,
            solid,
            quadrature_factor,
        )

    grid_shape = (4,) + control_porosity.shape
    adj = jnp.zeros(grid_shape, jnp.float32)
    for interior_block in range(device_instant_total - 1, -1, -1):
        adj, unused = one_step(adj, interior_block)
    adj = passed_along(adj, "arc", -1)
    partial_sum = jnp.zeros(control_porosity.shape, jnp.float32)
    for interior_block in range(device_instant_total - 1, -1, -1):
        adj, summand_contribution = one_step(adj, interior_block)
        partial_sum = partial_sum + summand_contribution
    summed = lax.psum(partial_sum, "arc")
    share = summed.shape[1] // lax.axis_size("arc")
    gradient = lax.dynamic_slice_in_dim(summed, lax.axis_index("arc") * share, share, 1)
    return (gradient, adj[None])


def swap_over(value, partner_bit):
    count = lax.axis_size("space")
    return lax.ppermute(value, "space", [(i, i ^ partner_bit) for i in range(count)])


def in_space_order(me, axis, own, near, far, relay):
    pieces = [own, near, far, relay]
    odd = (me & 1) == 1
    pieces = [
        jnp.where(odd, pieces[1], pieces[0]),
        jnp.where(odd, pieces[0], pieces[1]),
        jnp.where(odd, pieces[3], pieces[2]),
        jnp.where(odd, pieces[2], pieces[3]),
    ]
    high = (me & 2) == 2
    pieces = [
        jnp.where(high, pieces[2], pieces[0]),
        jnp.where(high, pieces[3], pieces[1]),
        jnp.where(high, pieces[0], pieces[2]),
        jnp.where(high, pieces[1], pieces[3]),
    ]
    return jnp.concatenate(pieces, axis=axis)


def gathered_cells(local, me, axis):
    near = swap_over(local, 1)
    far = swap_over(local, 2)
    relay = swap_over(far, 1)
    return in_space_order(me, axis, local, near, far, relay)


def whole_grid_body(
    saved_velocity_trajectory,
    saved_warmth_trajectory,
    control_porosity,
    control_volume_flag,
    entrance_face_flag,
):
    lanes = saved_warmth_trajectory.shape[1]
    steps = saved_warmth_trajectory.shape[0]
    me = lax.axis_index("space")

    stacked = jnp.concatenate(
        [saved_velocity_trajectory, saved_warmth_trajectory[:, None]], axis=1
    )
    inputs_all = [None] * steps
    chunk = 2 if steps % 2 == 0 else 1
    near_all = swap_over(stacked, 1)
    for top in range(steps, 0, -chunk):
        own = stacked[top - chunk:top]
        far = swap_over(own, 2)
        relay = swap_over(far, 1)
        piece = in_space_order(me, 2, own, near_all[top - chunk:top], far, relay)
        for j in range(chunk):
            inputs_all[top - chunk + j] = piece[j]

    own_gamma = jnp.where(control_volume_flag == 1, control_porosity, jnp.float32(0.0))
    gamma = gathered_cells(own_gamma, me, 0)
    solid = 1.0 - gamma
    alpha = 3.0 * 0.1 * solid / (0.1 + gamma)
    own_flag = control_volume_flag.astype(jnp.float32)
    own_sensitivity = -3.0 * 0.1 * 1.1 / ((0.1 + own_gamma) * (0.1 + own_gamma))

    def one_step(adj, s, a_zero=False):
        speed = inputs_all[s][:3].astype(jnp.float32)
        thermal = inputs_all[s][3].astype(jnp.float32)
        padded_thermal = jnp.pad(thermal, 1, mode="edge")
        ext_a = jnp.pad(adj[:3], ((0, 0), (1, 1), (1, 1), (1, 1)))
        b = adj[3]
        floor_limit = jnp.where(entrance_face_flag == 1, jnp.float32(0.0), b[0])
        ext_b = pad_sides(jnp.concatenate([floor_limit[None], b, b[-1][None]], axis=0), "edge")
        a_now = adj[:3]
        grad_b = slopes(ext_b)
        grad_a = slopes(ext_a)
        grad_t = slopes(padded_thermal)
        carry_b = speed[0] * grad_b[0] + speed[1] * grad_b[1] + speed[2] * grad_b[2]
        carry_a = speed[0:1] * grad_a[0] + speed[1:2] * grad_a[1] + speed[2:3] * grad_a[2]
        if a_zero:
            new_a = 0.1 * (0.0 - b * jnp.stack(grad_t))
        else:
            new_a = a_now + 0.1 * (
                1.2 * laplace(ext_a) + carry_a - alpha * a_now - b * jnp.stack(grad_t)
            )
        new_b = b + 0.1 * (1.2 * laplace(ext_b) + carry_b - 2.0 * solid * b + 2.0 * solid)
        return jnp.concatenate([new_a, new_b[None]], axis=0)

    def own_cells(x, axis):
        return lax.dynamic_slice_in_dim(x, me * lanes, lanes, axis)

    def sensitivity(adj, s):
        a_loc = own_cells(adj[:3], 1)
        b_loc = own_cells(adj[3], 0)
        speed = saved_velocity_trajectory[s].astype(jnp.float32)
        thermal = saved_warmth_trajectory[s].astype(jnp.float32)
        dot = jnp.sum(a_loc * speed, axis=0)
        return 0.1 * own_flag * (own_sensitivity * dot + 2.0 * (b_loc - 1.0) * thermal)

    grid_shape = (4,) + gamma.shape
    adj = jnp.concatenate(
        [jnp.zeros((3,) + gamma.shape, jnp.float32), (0.1 * (2.0 * solid))[None]], axis=0
    )
    for s in range(steps - 2, -1, -1):
        adj = one_step(adj, s, a_zero=(s == steps - 2))

    core = me % 2
    half = adj.shape[0] // 2
    mine = lax.dynamic_slice_in_dim(adj, core * half, half, 0)
    arrived = passed_along(mine, "arc", -1)
    space_count = lax.axis_size("space")
    swap = [(i, i ^ 1) for i in range(space_count)]
    other = lax.ppermute(arrived, "space", swap)
    adj = jnp.where(
        core == 0,
        jnp.concatenate([arrived, other], axis=0),
        jnp.concatenate([other, arrived], axis=0),
    )

    partial_sum = jnp.zeros(control_porosity.shape, jnp.float32)
    for s in range(steps - 1, -1, -1):
        partial_sum = partial_sum + sensitivity(adj, s)
        adj = one_step(adj, s)

    arcs = lax.axis_size("arc")
    k = lax.axis_index("arc")
    share = partial_sum.shape[1] // arcs
    pieces = partial_sum.reshape(partial_sum.shape[0], arcs, share, partial_sum.shape[2])
    total = lax.dynamic_index_in_dim(pieces, k, 1, keepdims=False)
    for shift in range(1, arcs):
        piece = lax.dynamic_index_in_dim(pieces, (k + shift) % arcs, 1, keepdims=False)
        total = total + passed_along(piece, "arc", shift)
    entry = own_cells(adj, 1)
    return (total, entry[None])


def solution(mesh):
    chosen = whole_grid_body if mesh.shape["space"] == 4 else halo_body
    return jax.shard_map(
        chosen,
        mesh=mesh,
        in_specs=(
            P(("job", "arc"), None, "space", None, None),
            P(("job", "arc"), "space", None, None),
            P(("job", "space"), None, None),
            P(("job", "space"), None, None),
            P("job", None),
        ),
        out_specs=(P(("job", "space"), "arc", None), P(("job", "arc"), None, "space", None, None)),
        check_vma=False,
    )
```

```python
import jax
import jax.numpy as jnp
from jax import lax
from jax.sharding import PartitionSpec as P


def padded(cells, sides, width):
    for axis, dim in sides:
        count = lax.axis_size(axis)
        ends = count - 1
        head = lax.slice_in_dim(cells, 0, width, axis=dim)
        tail = lax.slice_in_dim(cells, cells.shape[dim] - width, cells.shape[dim], axis=dim)
        cells = jnp.concatenate(
            [
                lax.ppermute(tail, axis, [(i, (i + 1) % count) for i in range(ends)]),
                cells,
                lax.ppermute(head, axis, [((i + 1) % count, i) for i in range(ends)]),
            ],
            axis=dim,
        )
    return cells


def passed_along(value, axis, steps):
    count = lax.axis_size(axis)
    pairs = [(source, (source + steps) % count) for source in range(count)]
    return lax.ppermute(value, axis, pairs)


def laplace(ext):
    mid = ext[..., 1:-1, 1:-1, 1:-1]
    total = ext[..., 2:, 1:-1, 1:-1] + ext[..., :-2, 1:-1, 1:-1]
    total = total + ext[..., 1:-1, 2:, 1:-1] + ext[..., 1:-1, :-2, 1:-1]
    total = total + ext[..., 1:-1, 1:-1, 2:] + ext[..., 1:-1, 1:-1, :-2]
    return total - 6.0 * mid


def slopes(ext):
    return (
        0.5 * (ext[..., 2:, 1:-1, 1:-1] - ext[..., :-2, 1:-1, 1:-1]),
        0.5 * (ext[..., 1:-1, 2:, 1:-1] - ext[..., 1:-1, :-2, 1:-1]),
        0.5 * (ext[..., 1:-1, 1:-1, 2:] - ext[..., 1:-1, 1:-1, :-2]),
    )


def pad_sides(field, operating_variant):
    widths = [(0, 0)] * (field.ndim - 2) + [(1, 1), (1, 1)]
    return jnp.pad(field, widths, mode=operating_variant)


def adjoint_update(
    adj,
    ext_a,
    ext_b,
    padded_thermal_field,
    speed,
    alpha,
    porosity_sensitivity,
    solid,
    quadrature_factor,
):
    a_now = adj[:3]
    current_adjoint_vector = adj[3]
    grad_b = slopes(ext_b)
    grad_a = slopes(ext_a)
    grad_t = slopes(padded_thermal_field)
    carry_b = speed[0] * grad_b[0] + speed[1] * grad_b[1] + speed[2] * grad_b[2]
    carry_a = speed[0:1] * grad_a[0] + speed[1:2] * grad_a[1] + speed[2:3] * grad_a[2]
    thermal_current_field = padded_thermal_field[1:-1, 1:-1, 1:-1]
    grad_stack = jnp.stack(grad_t)
    new_a = a_now + 0.1 * (
        1.2 * laplace(ext_a) + carry_a - alpha * a_now - current_adjoint_vector * grad_stack
    )
    new_b = current_adjoint_vector + 0.1 * (
        1.2 * laplace(ext_b) + carry_b - 2.0 * solid * current_adjoint_vector + 2.0 * solid
    )
    common_divisor_lcm_like = jnp.sum(a_now * speed, axis=0)
    summand_contribution = (
        0.1
        * quadrature_factor
        * (
            porosity_sensitivity * common_divisor_lcm_like
            + 2.0 * (current_adjoint_vector - 1.0) * thermal_current_field
        )
    )
    return (jnp.concatenate([new_a, new_b[None]], axis=0), summand_contribution)


def halo_body(
    saved_velocity_trajectory,
    saved_warmth_trajectory,
    control_porosity,
    control_volume_flag,
    entrance_face_flag,
):
    quadrature_factor = control_volume_flag.astype(jnp.float32)
    gamma = jnp.where(control_volume_flag == 1, control_porosity, jnp.float32(0.0))
    solid = 1.0 - gamma
    alpha = 3.0 * 0.1 * solid / (0.1 + gamma)
    porosity_sensitivity = -3.0 * 0.1 * 1.1 / ((0.1 + gamma) * (0.1 + gamma))
    leading_plane = lax.axis_index("space") == 0
    trailing_plane = lax.axis_index("space") == lax.axis_size("space") - 1
    device_instant_total = saved_warmth_trajectory.shape[0]
    cycle_ext = padded(saved_warmth_trajectory, (("space", 1),), 1)

    def closing_thermal_value(thermal_current_field, with_halo_padding):
        floor_limit = jnp.where(leading_plane, thermal_current_field[0], with_halo_padding[0])
        ceiling_bound = jnp.where(trailing_plane, thermal_current_field[-1], with_halo_padding[-1])
        return pad_sides(
            jnp.concatenate(
                [floor_limit[None], thermal_current_field, ceiling_bound[None]], axis=0
            ),
            "edge",
        )

    def one_step(adj, interior_block):
        speed = saved_velocity_trajectory[interior_block].astype(jnp.float32)
        thermal_current_field = saved_warmth_trajectory[interior_block].astype(jnp.float32)
        with_halo_padding = padded(adj, (("space", 1),), 1)
        thermal_halo_values = cycle_ext[interior_block].astype(jnp.float32)
        complete_thermal_field = jnp.concatenate(
            [thermal_halo_values[:1], thermal_current_field, thermal_halo_values[-1:]], axis=0
        )
        padded_thermal_field = closing_thermal_value(thermal_current_field, complete_thermal_field)
        ext_a = pad_sides(with_halo_padding[:3], "constant")
        current_adjoint_vector = adj[3]
        floor_limit = jnp.where(
            leading_plane,
            jnp.where(entrance_face_flag == 1, jnp.float32(0.0), current_adjoint_vector[0]),
            with_halo_padding[3, 0],
        )
        ceiling_bound = jnp.where(
            trailing_plane, current_adjoint_vector[-1], with_halo_padding[3, -1]
        )
        ext_b = pad_sides(
            jnp.concatenate(
                [floor_limit[None], current_adjoint_vector, ceiling_bound[None]], axis=0
            ),
            "edge",
        )
        return adjoint_update(
            adj,
            ext_a,
            ext_b,
            padded_thermal_field,
            speed,
            alpha,
            porosity_sensitivity,
            solid,
            quadrature_factor,
        )

    grid_shape = (4,) + control_porosity.shape
    adj = jnp.zeros(grid_shape, jnp.float32)
    for interior_block in range(device_instant_total - 1, -1, -1):
        adj, unused = one_step(adj, interior_block)
    adj = passed_along(adj, "arc", -1)
    partial_sum = jnp.zeros(control_porosity.shape, jnp.float32)
    for interior_block in range(device_instant_total - 1, -1, -1):
        adj, summand_contribution = one_step(adj, interior_block)
        partial_sum = partial_sum + summand_contribution
    summed = lax.psum(partial_sum, "arc")
    share = summed.shape[1] // lax.axis_size("arc")
    gradient = lax.dynamic_slice_in_dim(summed, lax.axis_index("arc") * share, share, 1)
    return (gradient, adj[None])


def swap_over(value, partner_bit):
    count = lax.axis_size("space")
    return lax.ppermute(value, "space", [(i, i ^ partner_bit) for i in range(count)])


def in_space_order(me, axis, own, near, far, relay):
    pieces = [own, near, far, relay]
    odd = (me & 1) == 1
    pieces = [
        jnp.where(odd, pieces[1], pieces[0]),
        jnp.where(odd, pieces[0], pieces[1]),
        jnp.where(odd, pieces[3], pieces[2]),
        jnp.where(odd, pieces[2], pieces[3]),
    ]
    high = (me & 2) == 2
    pieces = [
        jnp.where(high, pieces[2], pieces[0]),
        jnp.where(high, pieces[3], pieces[1]),
        jnp.where(high, pieces[0], pieces[2]),
        jnp.where(high, pieces[1], pieces[3]),
    ]
    return jnp.concatenate(pieces, axis=axis)


def gathered_cells(local, me, axis):
    near = swap_over(local, 1)
    far = swap_over(local, 2)
    relay = swap_over(far, 1)
    return in_space_order(me, axis, local, near, far, relay)


def whole_grid_body(
    saved_velocity_trajectory,
    saved_warmth_trajectory,
    control_porosity,
    control_volume_flag,
    entrance_face_flag,
):
    lanes = saved_warmth_trajectory.shape[1]
    steps = saved_warmth_trajectory.shape[0]
    me = lax.axis_index("space")

    stacked = jnp.concatenate(
        [saved_velocity_trajectory, saved_warmth_trajectory[:, None]], axis=1
    )
    inputs_all = [None] * steps
    chunk = 4 if steps % 4 == 0 else 1
    near_all = swap_over(stacked, 1)
    for top in range(steps, 0, -chunk):
        own = stacked[top - chunk:top]
        far = swap_over(own, 2)
        relay = swap_over(far, 1)
        piece = in_space_order(me, 2, own, near_all[top - chunk:top], far, relay)
        for j in range(chunk):
            inputs_all[top - chunk + j] = piece[j]

    own_gamma = jnp.where(control_volume_flag == 1, control_porosity, jnp.float32(0.0))
    gamma = gathered_cells(own_gamma, me, 0)
    solid = 1.0 - gamma
    alpha = 3.0 * 0.1 * solid / (0.1 + gamma)
    own_flag = control_volume_flag.astype(jnp.float32)
    own_sensitivity = -3.0 * 0.1 * 1.1 / ((0.1 + own_gamma) * (0.1 + own_gamma))

    def one_step(adj, s, a_zero=False):
        speed = inputs_all[s][:3].astype(jnp.float32)
        thermal = inputs_all[s][3].astype(jnp.float32)
        padded_thermal = jnp.pad(thermal, 1, mode="edge")
        ext_a = jnp.pad(adj[:3], ((0, 0), (1, 1), (1, 1), (1, 1)))
        b = adj[3]
        floor_limit = jnp.where(entrance_face_flag == 1, jnp.float32(0.0), b[0])
        ext_b = pad_sides(jnp.concatenate([floor_limit[None], b, b[-1][None]], axis=0), "edge")
        a_now = adj[:3]
        grad_b = slopes(ext_b)
        grad_a = slopes(ext_a)
        grad_t = slopes(padded_thermal)
        carry_b = speed[0] * grad_b[0] + speed[1] * grad_b[1] + speed[2] * grad_b[2]
        carry_a = speed[0:1] * grad_a[0] + speed[1:2] * grad_a[1] + speed[2:3] * grad_a[2]
        if a_zero:
            new_a = 0.1 * (0.0 - b * jnp.stack(grad_t))
        else:
            new_a = a_now + 0.1 * (
                1.2 * laplace(ext_a) + carry_a - alpha * a_now - b * jnp.stack(grad_t)
            )
        new_b = b + 0.1 * (1.2 * laplace(ext_b) + carry_b - 2.0 * solid * b + 2.0 * solid)
        return jnp.concatenate([new_a, new_b[None]], axis=0)

    def own_cells(x, axis):
        return lax.dynamic_slice_in_dim(x, me * lanes, lanes, axis)

    def sensitivity(adj, s):
        a_loc = own_cells(adj[:3], 1)
        b_loc = own_cells(adj[3], 0)
        speed = saved_velocity_trajectory[s].astype(jnp.float32)
        thermal = saved_warmth_trajectory[s].astype(jnp.float32)
        dot = jnp.sum(a_loc * speed, axis=0)
        return 0.1 * own_flag * (own_sensitivity * dot + 2.0 * (b_loc - 1.0) * thermal)

    grid_shape = (4,) + gamma.shape
    adj = jnp.concatenate(
        [jnp.zeros((3,) + gamma.shape, jnp.float32), (0.1 * (2.0 * solid))[None]], axis=0
    )
    for s in range(steps - 2, -1, -1):
        adj = one_step(adj, s, a_zero=(s == steps - 2))

    core = me % 2
    half = adj.shape[0] // 2
    mine = lax.dynamic_slice_in_dim(adj, core * half, half, 0)
    arrived = passed_along(mine, "arc", -1)
    space_count = lax.axis_size("space")
    swap = [(i, i ^ 1) for i in range(space_count)]
    other = lax.ppermute(arrived, "space", swap)
    adj = jnp.where(
        core == 0,
        jnp.concatenate([arrived, other], axis=0),
        jnp.concatenate([other, arrived], axis=0),
    )

    partial_sum = jnp.zeros(control_porosity.shape, jnp.float32)
    for s in range(steps - 1, -1, -1):
        partial_sum = partial_sum + sensitivity(adj, s)
        adj = one_step(adj, s)

    arcs = lax.axis_size("arc")
    k = lax.axis_index("arc")
    share = partial_sum.shape[1] // arcs
    pieces = partial_sum.reshape(partial_sum.shape[0], arcs, share, partial_sum.shape[2])
    total = lax.dynamic_index_in_dim(pieces, k, 1, keepdims=False)
    for shift in range(1, arcs):
        piece = lax.dynamic_index_in_dim(pieces, (k + shift) % arcs, 1, keepdims=False)
        total = total + passed_along(piece, "arc", shift)
    entry = own_cells(adj, 1)
    return (total, entry[None])


def solution(mesh):
    chosen = whole_grid_body if mesh.shape["space"] == 4 else halo_body
    return jax.shard_map(
        chosen,
        mesh=mesh,
        in_specs=(
            P(("job", "arc"), None, "space", None, None),
            P(("job", "arc"), "space", None, None),
            P(("job", "space"), None, None),
            P(("job", "space"), None, None),
            P("job", None),
        ),
        out_specs=(P(("job", "space"), "arc", None), P(("job", "arc"), None, "space", None, None)),
        check_vma=False,
    )
```

```python
import jax
import jax.numpy as jnp
from jax import lax
from jax.sharding import PartitionSpec as P


def padded(cells, sides, width):
    for axis, dim in sides:
        count = lax.axis_size(axis)
        ends = count - 1
        head = lax.slice_in_dim(cells, 0, width, axis=dim)
        tail = lax.slice_in_dim(cells, cells.shape[dim] - width, cells.shape[dim], axis=dim)
        cells = jnp.concatenate(
            [
                lax.ppermute(tail, axis, [(i, (i + 1) % count) for i in range(ends)]),
                cells,
                lax.ppermute(head, axis, [((i + 1) % count, i) for i in range(ends)]),
            ],
            axis=dim,
        )
    return cells


def passed_along(value, axis, steps):
    count = lax.axis_size(axis)
    pairs = [(source, (source + steps) % count) for source in range(count)]
    return lax.ppermute(value, axis, pairs)


def laplace(ext):
    mid = ext[..., 1:-1, 1:-1, 1:-1]
    total = ext[..., 2:, 1:-1, 1:-1] + ext[..., :-2, 1:-1, 1:-1]
    total = total + ext[..., 1:-1, 2:, 1:-1] + ext[..., 1:-1, :-2, 1:-1]
    total = total + ext[..., 1:-1, 1:-1, 2:] + ext[..., 1:-1, 1:-1, :-2]
    return total - 6.0 * mid


def slopes(ext):
    return (
        0.5 * (ext[..., 2:, 1:-1, 1:-1] - ext[..., :-2, 1:-1, 1:-1]),
        0.5 * (ext[..., 1:-1, 2:, 1:-1] - ext[..., 1:-1, :-2, 1:-1]),
        0.5 * (ext[..., 1:-1, 1:-1, 2:] - ext[..., 1:-1, 1:-1, :-2]),
    )


def pad_sides(field, operating_variant):
    widths = [(0, 0)] * (field.ndim - 2) + [(1, 1), (1, 1)]
    return jnp.pad(field, widths, mode=operating_variant)


def adjoint_update(
    adj,
    ext_a,
    ext_b,
    padded_thermal_field,
    speed,
    alpha,
    porosity_sensitivity,
    solid,
    quadrature_factor,
):
    a_now = adj[:3]
    current_adjoint_vector = adj[3]
    grad_b = slopes(ext_b)
    grad_a = slopes(ext_a)
    grad_t = slopes(padded_thermal_field)
    carry_b = speed[0] * grad_b[0] + speed[1] * grad_b[1] + speed[2] * grad_b[2]
    carry_a = speed[0:1] * grad_a[0] + speed[1:2] * grad_a[1] + speed[2:3] * grad_a[2]
    thermal_current_field = padded_thermal_field[1:-1, 1:-1, 1:-1]
    grad_stack = jnp.stack(grad_t)
    new_a = a_now + 0.1 * (
        1.2 * laplace(ext_a) + carry_a - alpha * a_now - current_adjoint_vector * grad_stack
    )
    new_b = current_adjoint_vector + 0.1 * (
        1.2 * laplace(ext_b) + carry_b - 2.0 * solid * current_adjoint_vector + 2.0 * solid
    )
    common_divisor_lcm_like = jnp.sum(a_now * speed, axis=0)
    summand_contribution = (
        0.1
        * quadrature_factor
        * (
            porosity_sensitivity * common_divisor_lcm_like
            + 2.0 * (current_adjoint_vector - 1.0) * thermal_current_field
        )
    )
    return (jnp.concatenate([new_a, new_b[None]], axis=0), summand_contribution)


def halo_body(
    saved_velocity_trajectory,
    saved_warmth_trajectory,
    control_porosity,
    control_volume_flag,
    entrance_face_flag,
):
    quadrature_factor = control_volume_flag.astype(jnp.float32)
    gamma = jnp.where(control_volume_flag == 1, control_porosity, jnp.float32(0.0))
    solid = 1.0 - gamma
    alpha = 3.0 * 0.1 * solid / (0.1 + gamma)
    porosity_sensitivity = -3.0 * 0.1 * 1.1 / ((0.1 + gamma) * (0.1 + gamma))
    leading_plane = lax.axis_index("space") == 0
    trailing_plane = lax.axis_index("space") == lax.axis_size("space") - 1
    device_instant_total = saved_warmth_trajectory.shape[0]
    cycle_ext = padded(saved_warmth_trajectory, (("space", 1),), 1)

    def closing_thermal_value(thermal_current_field, with_halo_padding):
        floor_limit = jnp.where(leading_plane, thermal_current_field[0], with_halo_padding[0])
        ceiling_bound = jnp.where(trailing_plane, thermal_current_field[-1], with_halo_padding[-1])
        return pad_sides(
            jnp.concatenate(
                [floor_limit[None], thermal_current_field, ceiling_bound[None]], axis=0
            ),
            "edge",
        )

    def one_step(adj, interior_block):
        speed = saved_velocity_trajectory[interior_block].astype(jnp.float32)
        thermal_current_field = saved_warmth_trajectory[interior_block].astype(jnp.float32)
        with_halo_padding = padded(adj, (("space", 1),), 1)
        thermal_halo_values = cycle_ext[interior_block].astype(jnp.float32)
        complete_thermal_field = jnp.concatenate(
            [thermal_halo_values[:1], thermal_current_field, thermal_halo_values[-1:]], axis=0
        )
        padded_thermal_field = closing_thermal_value(thermal_current_field, complete_thermal_field)
        ext_a = pad_sides(with_halo_padding[:3], "constant")
        current_adjoint_vector = adj[3]
        floor_limit = jnp.where(
            leading_plane,
            jnp.where(entrance_face_flag == 1, jnp.float32(0.0), current_adjoint_vector[0]),
            with_halo_padding[3, 0],
        )
        ceiling_bound = jnp.where(
            trailing_plane, current_adjoint_vector[-1], with_halo_padding[3, -1]
        )
        ext_b = pad_sides(
            jnp.concatenate(
                [floor_limit[None], current_adjoint_vector, ceiling_bound[None]], axis=0
            ),
            "edge",
        )
        return adjoint_update(
            adj,
            ext_a,
            ext_b,
            padded_thermal_field,
            speed,
            alpha,
            porosity_sensitivity,
            solid,
            quadrature_factor,
        )

    grid_shape = (4,) + control_porosity.shape
    adj = jnp.zeros(grid_shape, jnp.float32)
    for interior_block in range(device_instant_total - 1, -1, -1):
        adj, unused = one_step(adj, interior_block)
    adj = passed_along(adj, "arc", -1)
    partial_sum = jnp.zeros(control_porosity.shape, jnp.float32)
    for interior_block in range(device_instant_total - 1, -1, -1):
        adj, summand_contribution = one_step(adj, interior_block)
        partial_sum = partial_sum + summand_contribution
    summed = lax.psum(partial_sum, "arc")
    share = summed.shape[1] // lax.axis_size("arc")
    gradient = lax.dynamic_slice_in_dim(summed, lax.axis_index("arc") * share, share, 1)
    return (gradient, adj[None])


def swap_over(value, partner_bit):
    count = lax.axis_size("space")
    return lax.ppermute(value, "space", [(i, i ^ partner_bit) for i in range(count)])


def in_space_order(me, axis, own, near, far, relay):
    pieces = [own, near, far, relay]
    odd = (me & 1) == 1
    pieces = [
        jnp.where(odd, pieces[1], pieces[0]),
        jnp.where(odd, pieces[0], pieces[1]),
        jnp.where(odd, pieces[3], pieces[2]),
        jnp.where(odd, pieces[2], pieces[3]),
    ]
    high = (me & 2) == 2
    pieces = [
        jnp.where(high, pieces[2], pieces[0]),
        jnp.where(high, pieces[3], pieces[1]),
        jnp.where(high, pieces[0], pieces[2]),
        jnp.where(high, pieces[1], pieces[3]),
    ]
    return jnp.concatenate(pieces, axis=axis)


def gathered_cells(local, me, axis):
    near = swap_over(local, 1)
    far = swap_over(local, 2)
    relay = swap_over(far, 1)
    return in_space_order(me, axis, local, near, far, relay)


def whole_grid_body(
    saved_velocity_trajectory,
    saved_warmth_trajectory,
    control_porosity,
    control_volume_flag,
    entrance_face_flag,
):
    lanes = saved_warmth_trajectory.shape[1]
    steps = saved_warmth_trajectory.shape[0]
    me = lax.axis_index("space")

    stacked = jnp.concatenate(
        [saved_velocity_trajectory, saved_warmth_trajectory[:, None]], axis=1
    )
    inputs_all = [None] * steps
    chunk = 2 if steps % 2 == 0 else 1
    near_all = swap_over(stacked, 1)
    for top in range(steps, 0, -chunk):
        own = stacked[top - chunk:top]
        far = swap_over(own, 2)
        relay = swap_over(far, 1)
        piece = in_space_order(me, 2, own, near_all[top - chunk:top], far, relay)
        for j in range(chunk):
            inputs_all[top - chunk + j] = piece[j]

    own_gamma = jnp.where(control_volume_flag == 1, control_porosity, jnp.float32(0.0))
    gamma = gathered_cells(own_gamma, me, 0)
    solid = 1.0 - gamma
    alpha = 3.0 * 0.1 * solid / (0.1 + gamma)
    own_flag = control_volume_flag.astype(jnp.float32)
    own_sensitivity = -3.0 * 0.1 * 1.1 / ((0.1 + own_gamma) * (0.1 + own_gamma))

    def one_step(adj, s, a_zero=False, own_only=False):
        speed = inputs_all[s][:3].astype(jnp.float32)
        thermal = inputs_all[s][3].astype(jnp.float32)
        padded_thermal = jnp.pad(thermal, 1, mode="edge")
        ext_a = jnp.pad(adj[:3], ((0, 0), (1, 1), (1, 1), (1, 1)))
        b = adj[3]
        floor_limit = jnp.where(entrance_face_flag == 1, jnp.float32(0.0), b[0])
        ext_b = pad_sides(jnp.concatenate([floor_limit[None], b, b[-1][None]], axis=0), "edge")
        a_now = adj[:3]
        alpha_s, solid_s = alpha, solid
        if own_only:
            near_cells = lambda x, axis: lax.dynamic_slice_in_dim(x, me * lanes, lanes + 2, axis)
            padded_thermal = near_cells(padded_thermal, 0)
            ext_a = near_cells(ext_a, 1)
            ext_b = near_cells(ext_b, 0)
            speed = own_cells(speed, 1)
            a_now = own_cells(a_now, 1)
            b = own_cells(b, 0)
            alpha_s, solid_s = own_cells(alpha, 0), own_cells(solid, 0)
        grad_b = slopes(ext_b)
        grad_a = slopes(ext_a)
        grad_t = slopes(padded_thermal)
        carry_b = speed[0] * grad_b[0] + speed[1] * grad_b[1] + speed[2] * grad_b[2]
        carry_a = speed[0:1] * grad_a[0] + speed[1:2] * grad_a[1] + speed[2:3] * grad_a[2]
        if a_zero:
            new_a = 0.1 * (0.0 - b * jnp.stack(grad_t))
        else:
            new_a = a_now + 0.1 * (
                1.2 * laplace(ext_a) + carry_a - alpha_s * a_now - b * jnp.stack(grad_t)
            )
        new_b = b + 0.1 * (1.2 * laplace(ext_b) + carry_b - 2.0 * solid_s * b + 2.0 * solid_s)
        return jnp.concatenate([new_a, new_b[None]], axis=0)

    def own_cells(x, axis):
        return lax.dynamic_slice_in_dim(x, me * lanes, lanes, axis)

    def sensitivity(adj, s):
        a_loc = own_cells(adj[:3], 1)
        b_loc = own_cells(adj[3], 0)
        speed = saved_velocity_trajectory[s].astype(jnp.float32)
        thermal = saved_warmth_trajectory[s].astype(jnp.float32)
        dot = jnp.sum(a_loc * speed, axis=0)
        return 0.1 * own_flag * (own_sensitivity * dot + 2.0 * (b_loc - 1.0) * thermal)

    grid_shape = (4,) + gamma.shape
    adj = jnp.concatenate(
        [jnp.zeros((3,) + gamma.shape, jnp.float32), (0.1 * (2.0 * solid))[None]], axis=0
    )
    for s in range(steps - 2, -1, -1):
        adj = one_step(adj, s, a_zero=(s == steps - 2))

    core = me % 2
    half = adj.shape[0] // 2
    mine = lax.dynamic_slice_in_dim(adj, core * half, half, 0)
    arrived = passed_along(mine, "arc", -1)
    space_count = lax.axis_size("space")
    swap = [(i, i ^ 1) for i in range(space_count)]
    other = lax.ppermute(arrived, "space", swap)
    adj = jnp.where(
        core == 0,
        jnp.concatenate([arrived, other], axis=0),
        jnp.concatenate([other, arrived], axis=0),
    )

    partial_sum = jnp.zeros(control_porosity.shape, jnp.float32)
    for s in range(steps - 1, -1, -1):
        partial_sum = partial_sum + sensitivity(adj, s)
        adj = one_step(adj, s, own_only=(s == 0))

    arcs = lax.axis_size("arc")
    k = lax.axis_index("arc")
    share = partial_sum.shape[1] // arcs
    pieces = partial_sum.reshape(partial_sum.shape[0], arcs, share, partial_sum.shape[2])
    total = lax.dynamic_index_in_dim(pieces, k, 1, keepdims=False)
    for shift in range(1, arcs):
        piece = lax.dynamic_index_in_dim(pieces, (k + shift) % arcs, 1, keepdims=False)
        total = total + passed_along(piece, "arc", shift)
    entry = adj
    return (total, entry[None])


def solution(mesh):
    chosen = whole_grid_body if mesh.shape["space"] == 4 else halo_body
    return jax.shard_map(
        chosen,
        mesh=mesh,
        in_specs=(
            P(("job", "arc"), None, "space", None, None),
            P(("job", "arc"), "space", None, None),
            P(("job", "space"), None, None),
            P(("job", "space"), None, None),
            P("job", None),
        ),
        out_specs=(P(("job", "space"), "arc", None), P(("job", "arc"), None, "space", None, None)),
        check_vma=False,
    )
```
